512 devices in a mesh: seq: 64 (over y, z), tp: 8 (over x, core).
Axes of the slice: x: 4, y: 4, z: 16, core: 2. Of those that a mesh axis runs over, the one named last changes fastest.
Arguments:
- tokens: bfloat16 [1088, 2048], P('seq'), may hold values from -6 to 6
- norm_gain: bfloat16 [2048], replicated, may hold values from 0.099609375 to 1.8984375
- w_query: bfloat16 [2048, 2048], P(None, 'tp'), may hold values from -0.125 to 0.125
- w_key: bfloat16 [2048, 1024], P(None, 'tp'), may hold values from -0.125 to 0.125
- w_value: bfloat16 [2048, 1024], P(None, 'tp'), may hold values from -0.125 to 0.125
- w_out: bfloat16 [2048, 2048], P('tp'), may hold values from -0.125 to 0.125
- cache_keys: bfloat16 [131072, 1024], P('seq', 'tp'), may hold values from -400 to 400
- cache_values: bfloat16 [131072, 1024], P('seq', 'tp'), may hold values from -6 to 6
- cached_len: int32 [66], replicated, may hold values from 1 to 16384, 131072 in all
- block_of_shard: int32 [64], P('seq'), may hold values from 0 to 63, each once
Outputs:
- mixed: bfloat16 [1088, 2048], P('seq', 'tp')
The draws below stay inside these ranges and needn't reach their ends.
Inputs may be any that keep to these rules, and one draw needn't show every extreme that they name: `cached_len`: they sum to exactly 131072, so every cache slot belongs to a request; the largest is 16384. `block_of_shard`: each index of seq stores a different block.
All inputs are finite; a program needn't handle non-finite values.
Results may differ from the reference program's by a relative error of at most 0.02.
Values may be sent and summed in bfloat16 or wider, within the bound.
No kernel may reach another device: no remote copies, remote signals or barrier semaphores. Data moves between devices by JAX's collectives and lax.ppermute only.
A program may use at most 192 MiB of HBM per device.

```python
import math
import jax
import jax.numpy as jnp
import numpy as np
from jax import lax

D = 2048
HQ = 16
KVH = 8
HD = 128
SPAN = 512
PREFILLS = 2
DECODES = 64
CACHE_DEV = 2048
NEW = 1088
REQS = 66
CACHE_ROWS = 131072
MAXLEN = 16384
N_SEQ = 64


def draw_cache_keys(key, part):
    first_key = jax.random.fold_in(key, 0)
    width_all = KVH * HD
    result = 1.5 * jax.random.normal(first_key, (CACHE_ROWS, width_all), jnp.float32)
    return result.astype(jnp.bfloat16)


def levels(own_key, extent, cuts, least, largest):
    loudness = 1.0
    for dim, parts in cuts:
        steps = jax.random.uniform(jax.random.fold_in(jax.random.fold_in(own_key, 6), dim), (parts,), jnp.float32, least / len(cuts), largest / len(cuts))
        loudness = loudness * jnp.repeat(jnp.exp(steps), extent[dim] // parts).reshape((-1,) + (1,) * (len(extent) - 1 - dim))
    return loudness


def length_profile(number_of, total, bound, slope):
    portions = [(1 << 20) // math.isqrt(rank ** slope) + 1 for rank in range(2, number_of + 1)]
    spare, counts = total - bound - (number_of - 1), [1] * (number_of - 1)
    while spare > 0:
        movable = [i for i in range(number_of - 1) if counts[i] < bound]
        whole, remaining = sum([portions[i] for i in movable]), spare
        for i in movable:
            more = min(bound - counts[i], max(1, remaining * portions[i] // whole), spare)
            counts[i] = counts[i] + more
            spare = spare - more
    return np.array([bound] + counts)


def ragged(own_key, number_of, total, bound, slope):
    if number_of == 2:
        one = jax.random.randint(own_key, (), max(1, total - bound), min(bound, total - 1) + 1)
        return jnp.stack([one, total - one])
    tallies = jnp.asarray(length_profile(number_of, total, bound, slope), jnp.int32)
    pairs = (number_of - 1) // 2
    giver, receiver = tallies[1:1 + 2 * pairs:2], tallies[2:2 + 2 * pairs:2]
    slack = jnp.minimum(giver - 1, bound - receiver)
    passed = jax.random.randint(jax.random.fold_in(own_key, 1), (pairs,), 0, 1 << 20) % (slack + 1)
    tallies = tallies.at[1:1 + 2 * pairs:2].set(giver - passed).at[2:2 + 2 * pairs:2].set(receiver + passed)
    return tallies[jax.random.permutation(jax.random.fold_in(own_key, 2), number_of)]


def bell_draw(own_key, dims, spread, bound, cuts=(), kind=jnp.bfloat16):
    drawn = spread * jax.random.normal(own_key, dims, jnp.float32)
    if cuts:
        drawn = drawn * levels(own_key, dims, cuts, -0.22, 0.18)
    return jnp.clip(drawn, -bound, bound).astype(kind)


def setup_inputs(seed: int = 0) -> dict:
    keys = jax.random.split(jax.random.key(seed), 11)
    return {
        "tokens": bell_draw(keys[0], (NEW, D), 1.0, 6.0, ((0, 64),)),
        "norm_gain": jnp.clip(1.0 + 0.18 * jax.random.normal(keys[1], (D,), jnp.float32), 0.099609375, 1.8984375).astype(jnp.bfloat16),
        "w_query": bell_draw(keys[2], (D, HQ * HD), D ** -0.5, 0.125, ((1, 8),)),
        "w_key": bell_draw(keys[3], (D, KVH * HD), D ** -0.5, 0.125, ((1, 8),)),
        "w_value": bell_draw(keys[4], (D, KVH * HD), D ** -0.5, 0.125, ((1, 8),)),
        "w_out": bell_draw(keys[5], (HQ * HD, D), (HQ * HD) ** -0.5, 0.125, ((0, 8),)),
        "cache_keys": draw_cache_keys(jax.random.fold_in(keys[10], 71), 0),
        "cache_values": bell_draw(keys[7], (CACHE_ROWS, KVH * HD), 1.0, 6.0, ((0, 64), (1, 8))),
        "cached_len": ragged(keys[8], REQS, CACHE_ROWS, MAXLEN, 2).astype(jnp.int32),
        "block_of_shard": jax.random.permutation(keys[9], N_SEQ).astype(jnp.int32),
    }


NEGATIVE = -1e+30
THETA = 1000000.0
EPSILON = 1e-06

def rotate(values, places):
    half_dim = values.shape[-1] // 2
    frequency = THETA ** (-jnp.arange(half_dim, dtype=jnp.float32) / half_dim)
    angles = places.astype(jnp.float32)[:, None] * frequency[None, :]
    cosine = jnp.cos(angles)[:, None, :]
    sine_part = jnp.sin(angles)[:, None, :]
    front_half = values[..., :half_dim]
    second = values[..., half_dim:]
    return jnp.concatenate([front_half * cosine - second * sine_part, second * cosine + front_half * sine_part], axis=-1)

def row_layout(row_count, cached_len):
    position_index = jnp.arange(row_count, dtype=jnp.int32)
    boundary = PREFILLS * SPAN
    request = jnp.where(position_index < boundary, position_index // SPAN, PREFILLS + position_index - boundary)
    offset = jnp.where(position_index < boundary, position_index % SPAN, 0)
    request = request.astype(jnp.int32)
    return (request, (jnp.take(cached_len, request) + offset).astype(jnp.int32))

def reference(tokens, norm_gain, w_query, w_key, w_value, w_out, cache_keys, cache_values, cached_len, block_of_shard):
    request, places = row_layout(NEW, cached_len)
    hidden = tokens.astype(jnp.float32)
    scale_row = lax.rsqrt(lax.optimization_barrier(jnp.mean(hidden * hidden, axis=1, keepdims=True)) + EPSILON)
    normed = (hidden * scale_row * norm_gain.astype(jnp.float32)[None, :]).astype(jnp.bfloat16)
    queries = jnp.dot(normed, w_query, preferred_element_type=jnp.float32).reshape(NEW, HQ, HD)
    queries = lax.optimization_barrier(rotate(queries, places).astype(jnp.bfloat16))
    new_keys = jnp.dot(normed, w_key, preferred_element_type=jnp.float32).reshape(NEW, KVH, HD)
    new_keys = lax.optimization_barrier(rotate(new_keys, places).astype(jnp.bfloat16))
    new_values = lax.optimization_barrier(jnp.dot(normed, w_value, preferred_element_type=jnp.float32).astype(jnp.bfloat16))
    new_k32 = new_keys.astype(jnp.float32)
    new_v32 = new_values.reshape(NEW, KVH, HD).astype(jnp.float32)
    owner = jnp.argsort(block_of_shard).astype(jnp.int32)
    padding = jnp.zeros((MAXLEN, KVH, HD), jnp.float32)
    packed_keys = cache_keys.reshape(N_SEQ, CACHE_DEV, KVH * HD)[owner].reshape(CACHE_ROWS, KVH, HD).astype(jnp.float32)
    packed_keys = jnp.concatenate([packed_keys, padding], axis=0)
    packed_values = cache_values.reshape(N_SEQ, CACHE_DEV, KVH * HD)[owner].reshape(CACHE_ROWS, KVH, HD).astype(jnp.float32)
    packed_values = jnp.concatenate([packed_values, padding], axis=0)
    starts = (jnp.cumsum(cached_len) - cached_len).astype(jnp.int32)
    groups = HQ // KVH

    def attend(block_item):
        q_block, req_one, pos_block = block_item
        begin = jnp.take(starts, req_one)
        length = jnp.take(cached_len, req_one)
        cache_k = lax.dynamic_slice_in_dim(packed_keys, begin, MAXLEN, 0)
        cache_v = lax.dynamic_slice_in_dim(packed_values, begin, MAXLEN, 0)
        rows_here = q_block.shape[0]
        q_four = q_block.astype(jnp.float32).reshape(rows_here, KVH, groups, HD)
        cache_scores = jnp.einsum('bcgd,kcd->bcgk', q_four, cache_k) * HD ** (-0.5)
        new_scores = jnp.einsum('bcgd,kcd->bcgk', q_four, new_k32) * HD ** (-0.5)
        cache_ok = jnp.broadcast_to((jnp.arange(MAXLEN, dtype=jnp.int32) < length)[None, :], (rows_here, MAXLEN))
        new_ok = (request[None, :] == req_one) & (places[None, :] <= pos_block[:, None])
        visible = jnp.concatenate([cache_ok, new_ok], axis=1)[:, None, None, :]
        scores = jnp.where(visible, jnp.concatenate([cache_scores, new_scores], axis=-1), NEGATIVE)
        row_top = lax.optimization_barrier(jnp.max(scores, axis=-1))
        weights = jnp.where(visible, jnp.exp(scores - row_top[..., None]), 0.0)
        denominator = lax.optimization_barrier(jnp.sum(weights, axis=-1))
        rounded = lax.optimization_barrier(weights.astype(jnp.bfloat16)).astype(jnp.float32)
        numerator = jnp.einsum('bcgk,kcd->bcgd', rounded[..., :MAXLEN], cache_v)
        numerator = numerator + jnp.einsum('bcgk,kcd->bcgd', rounded[..., MAXLEN:], new_v32)
        return (numerator / denominator[..., None]).astype(jnp.bfloat16).reshape(rows_here, HQ * HD)
    boundary = PREFILLS * SPAN
    sub_rows = min(SPAN, 128)
    pieces = SPAN // sub_rows
    flat_q = queries.reshape(NEW, HQ * HD)
    prefill_q = flat_q[:boundary].reshape(PREFILLS * pieces, sub_rows, HQ * HD)
    prefill_places = places[:boundary].reshape(PREFILLS * pieces, sub_rows)
    prefill_request = jnp.repeat(jnp.arange(PREFILLS, dtype=jnp.int32), pieces).astype(jnp.int32)
    prefill_out = lax.map(attend, (prefill_q, prefill_request, prefill_places))
    decode_q = flat_q[boundary:].reshape(DECODES, 1, HQ * HD)
    decode_places = places[boundary:].reshape(DECODES, 1)
    decode_request = (PREFILLS + jnp.arange(DECODES, dtype=jnp.int32)).astype(jnp.int32)
    decode_out = lax.map(attend, (decode_q, decode_request, decode_places))
    attended = jnp.concatenate([prefill_out.reshape(boundary, HQ * HD), decode_out.reshape(DECODES, HQ * HD)], axis=0)
    return jnp.dot(attended, w_out, preferred_element_type=jnp.float32).astype(jnp.bfloat16)
```

```python
import jax
import jax.numpy as jnp
from jax import lax
from jax.sharding import Mesh, PartitionSpec as P

HD = 128
SPAN = 512
PREFILLS = 2


SEQ = ("seq_hi", "seq_lo")
NEGATIVE = -1e30
THETA = 1000000.0
EPSILON = 1e-06


def rotate(values, places):
    half_dim = values.shape[-1] // 2
    frequency = THETA ** (-jnp.arange(half_dim, dtype=jnp.float32) / half_dim)
    angles = places.astype(jnp.float32)[:, None] * frequency[None, :]
    cosine = jnp.cos(angles)[:, None, :]
    sine_part = jnp.sin(angles)[:, None, :]
    front_half = values[..., :half_dim]
    second = values[..., half_dim:]
    return jnp.concatenate(
        [front_half * cosine - second * sine_part, second * cosine + front_half * sine_part],
        axis=-1,
    )


def row_layout(row_count, cached_len):
    position_index = jnp.arange(row_count, dtype=jnp.int32)
    boundary = PREFILLS * SPAN
    request = jnp.where(
        position_index < boundary, position_index // SPAN, PREFILLS + position_index - boundary
    )
    offset = jnp.where(position_index < boundary, position_index % SPAN, 0)
    matches = request[:, None] == jnp.arange(cached_len.shape[0], dtype=jnp.int32)[None, :]
    begins = jnp.sum(jnp.where(matches, cached_len[None, :], 0), axis=1)
    return (request, begins + offset)


def slot_layout(block_number, slot_count, cached_len):
    packed = block_number * slot_count + jnp.arange(slot_count, dtype=jnp.int32)
    ending = jnp.cumsum(cached_len)
    before = packed[:, None] >= ending[None, :]
    request = jnp.sum(before.astype(jnp.int32), axis=1)
    places = packed - jnp.sum(jnp.where(before, cached_len[None, :], 0), axis=1)
    return (request, places)


def per_device(
    tokens,
    norm_gain,
    w_query,
    w_key,
    w_value,
    w_out,
    cache_keys,
    cache_values,
    cached_len,
    block_of_shard,
):
    seq_count = lax.axis_size(SEQ)
    seq_index = lax.axis_index(SEQ)
    tok_rows = tokens.shape[0]
    all_rows = tok_rows * seq_count
    q_heads = w_query.shape[1] // HD
    kv_heads = w_key.shape[1] // HD
    head_groups = q_heads // kv_heads
    boundary = PREFILLS * SPAN
    request_all, position_all = row_layout(all_rows, cached_len)
    my_request = lax.dynamic_slice_in_dim(request_all, seq_index * tok_rows, tok_rows)
    my_position = lax.dynamic_slice_in_dim(position_all, seq_index * tok_rows, tok_rows)
    hidden = tokens.astype(jnp.float32)
    scale_row = lax.rsqrt(jnp.mean(hidden * hidden, axis=1, keepdims=True) + EPSILON)
    normed = (hidden * scale_row * norm_gain.astype(jnp.float32)[None, :]).astype(jnp.bfloat16)
    queries = jnp.dot(normed, w_query, preferred_element_type=jnp.float32).reshape(
        tok_rows, q_heads, HD
    )
    queries = rotate(queries, my_position).astype(jnp.bfloat16).reshape(tok_rows, q_heads * HD)
    new_keys = jnp.dot(normed, w_key, preferred_element_type=jnp.float32).reshape(
        tok_rows, kv_heads, HD
    )
    new_keys = rotate(new_keys, my_position).astype(jnp.bfloat16)
    new_values = (
        jnp.dot(normed, w_value, preferred_element_type=jnp.float32)
        .astype(jnp.bfloat16)
        .reshape(tok_rows, kv_heads, HD)
    )
    key_block = jnp.concatenate([cache_keys.reshape(-1, kv_heads, HD), new_keys], axis=0)
    value_block = jnp.concatenate([cache_values.reshape(-1, kv_heads, HD), new_values], axis=0)
    slot_request, slot_position = slot_layout(block_of_shard[0], cache_keys.shape[0], cached_len)
    key_request = jnp.concatenate([slot_request, my_request], axis=0)
    key_position = jnp.concatenate([slot_position, my_position], axis=0)
    gathered = lax.all_gather(
        lax.all_gather(queries, SEQ[1], axis=0, tiled=True), SEQ[0], axis=0, tiled=True
    )

    def block_partial(block_item):
        q_rows, q_request, q_position = block_item
        row_count = q_rows.shape[0]
        q_four = q_rows.reshape(row_count, kv_heads, head_groups, HD)
        scores = jnp.einsum(
            "bcgd,kcd->bcgk", q_four, key_block, preferred_element_type=jnp.float32
        ) * HD ** (-0.5)
        visible = (q_request[:, None] == key_request[None, :]) & (
            key_position[None, :] <= q_position[:, None]
        )
        visible = visible[:, None, None, :]
        scores = jnp.where(visible, scores, NEGATIVE)
        row_top = jnp.max(scores, axis=-1)
        weights = jnp.where(visible, jnp.exp(scores - row_top[..., None]), 0.0)
        denominator = jnp.sum(weights, axis=-1)
        numerator = jnp.einsum(
            "bcgk,kcd->bcgd",
            weights.astype(jnp.bfloat16),
            value_block,
            preferred_element_type=jnp.float32,
        )
        return (
            row_top.reshape(row_count, q_heads),
            numerator.reshape(row_count, q_heads, HD),
            denominator.reshape(row_count, q_heads),
        )

    def prefill_block(block_item):
        return block_partial(block_item)

    prefill_parts = lax.map(
        prefill_block,
        (
            gathered[:boundary].reshape(PREFILLS, SPAN, q_heads * HD),
            request_all[:boundary].reshape(PREFILLS, SPAN),
            position_all[:boundary].reshape(PREFILLS, SPAN),
        ),
    )
    decode_parts = block_partial(
        (gathered[boundary:], request_all[boundary:], position_all[boundary:])
    )
    row_top = jnp.concatenate(
        [prefill_parts[0].reshape(boundary, q_heads), decode_parts[0]], axis=0
    )
    numerator = jnp.concatenate(
        [prefill_parts[1].reshape(boundary, q_heads, HD), decode_parts[1]], axis=0
    )
    denominator = jnp.concatenate(
        [prefill_parts[2].reshape(boundary, q_heads), decode_parts[2]], axis=0
    )
    part_width = q_heads * (HD + 2)
    packed = jnp.concatenate(
        [numerator, denominator[..., None], row_top[..., None]], axis=-1
    ).reshape(seq_count, tok_rows * part_width)
    received = lax.all_to_all(packed, SEQ, 0, 0, tiled=True).reshape(
        seq_count, tok_rows, q_heads, HD + 2
    )
    part_top = received[..., HD + 1]
    overall = jnp.max(part_top, axis=0)
    factor = jnp.exp(part_top - overall[None])
    numerator = jnp.sum(received[..., :HD] * factor[..., None], axis=0)
    denominator = jnp.sum(received[..., HD] * factor, axis=0)
    attended = (
        (numerator / denominator[..., None]).astype(jnp.bfloat16).reshape(tok_rows, q_heads * HD)
    )
    partial_out = jnp.dot(attended, w_out, preferred_element_type=jnp.float32)
    return lax.psum_scatter(partial_out.astype(jnp.bfloat16), "tp", scatter_dimension=1, tiled=True)


def split_mesh(mesh):
    seq_devices = mesh.devices[:, 0]
    try:
        hi = len({d.coords[1] for d in seq_devices})
    except AttributeError:
        hi = 4
    if seq_devices.shape[0] % hi:
        hi = 1
    lo = seq_devices.shape[0] // hi
    grid = mesh.devices.reshape(hi, lo, mesh.devices.shape[1])
    return Mesh(grid, (SEQ[0], SEQ[1], "tp"))


def solution(mesh):
    split = split_mesh(mesh)
    in_specs = (
        P(SEQ, None),
        P(),
        P(None, "tp"),
        P(None, "tp"),
        P(None, "tp"),
        P("tp", None),
        P(SEQ, "tp"),
        P(SEQ, "tp"),
        P(),
        P(SEQ),
    )
    out_specs = P(SEQ, "tp")
    return jax.shard_map(
        per_device, mesh=split, in_specs=in_specs, out_specs=out_specs, check_vma=False
    )
```

```python
import jax
import jax.numpy as jnp
from jax import lax
from jax.sharding import Mesh, PartitionSpec as P

HD = 128
SPAN = 512
PREFILLS = 2


SEQ = ("seq_hi", "seq_lo")
NEGATIVE = -1e30
THETA = 1000000.0
EPSILON = 1e-06


def rotate(values, places):
    half_dim = values.shape[-1] // 2
    frequency = THETA ** (-jnp.arange(half_dim, dtype=jnp.float32) / half_dim)
    angles = places.astype(jnp.float32)[:, None] * frequency[None, :]
    cosine = jnp.cos(angles)[:, None, :]
    sine_part = jnp.sin(angles)[:, None, :]
    front_half = values[..., :half_dim]
    second = values[..., half_dim:]
    return jnp.concatenate(
        [front_half * cosine - second * sine_part, second * cosine + front_half * sine_part],
        axis=-1,
    )


def row_layout(row_count, cached_len):
    position_index = jnp.arange(row_count, dtype=jnp.int32)
    boundary = PREFILLS * SPAN
    request = jnp.where(
        position_index < boundary, position_index // SPAN, PREFILLS + position_index - boundary
    )
    offset = jnp.where(position_index < boundary, position_index % SPAN, 0)
    matches = request[:, None] == jnp.arange(cached_len.shape[0], dtype=jnp.int32)[None, :]
    begins = jnp.sum(jnp.where(matches, cached_len[None, :], 0), axis=1)
    return (request, begins + offset)


def slot_layout(block_number, slot_count, cached_len):
    packed = block_number * slot_count + jnp.arange(slot_count, dtype=jnp.int32)
    ending = jnp.cumsum(cached_len)
    before = packed[:, None] >= ending[None, :]
    request = jnp.sum(before.astype(jnp.int32), axis=1)
    places = packed - jnp.sum(jnp.where(before, cached_len[None, :], 0), axis=1)
    return (request, places)


def per_device(
    tokens,
    norm_gain,
    w_query,
    w_key,
    w_value,
    w_out,
    cache_keys,
    cache_values,
    cached_len,
    block_of_shard,
):
    seq_count = lax.axis_size(SEQ)
    seq_index = lax.axis_index(SEQ)
    tok_rows = tokens.shape[0]
    all_rows = tok_rows * seq_count
    q_heads = w_query.shape[1] // HD
    kv_heads = w_key.shape[1] // HD
    head_groups = q_heads // kv_heads
    boundary = PREFILLS * SPAN
    request_all, position_all = row_layout(all_rows, cached_len)
    my_request = lax.dynamic_slice_in_dim(request_all, seq_index * tok_rows, tok_rows)
    my_position = lax.dynamic_slice_in_dim(position_all, seq_index * tok_rows, tok_rows)
    hidden = tokens.astype(jnp.float32)
    scale_row = lax.rsqrt(jnp.mean(hidden * hidden, axis=1, keepdims=True) + EPSILON)
    normed = (hidden * scale_row * norm_gain.astype(jnp.float32)[None, :]).astype(jnp.bfloat16)
    queries = jnp.dot(normed, w_query, preferred_element_type=jnp.float32).reshape(
        tok_rows, q_heads, HD
    )
    queries = rotate(queries, my_position).astype(jnp.bfloat16).reshape(tok_rows, q_heads * HD)
    new_keys = jnp.dot(normed, w_key, preferred_element_type=jnp.float32).reshape(
        tok_rows, kv_heads, HD
    )
    new_keys = rotate(new_keys, my_position).astype(jnp.bfloat16)
    new_values = (
        jnp.dot(normed, w_value, preferred_element_type=jnp.float32)
        .astype(jnp.bfloat16)
        .reshape(tok_rows, kv_heads, HD)
    )
    key_block = jnp.concatenate([cache_keys.reshape(-1, kv_heads, HD), new_keys], axis=0)
    value_block = jnp.concatenate([cache_values.reshape(-1, kv_heads, HD), new_values], axis=0)
    slot_request, slot_position = slot_layout(block_of_shard[0], cache_keys.shape[0], cached_len)
    key_request = jnp.concatenate([slot_request, my_request], axis=0)
    key_position = jnp.concatenate([slot_position, my_position], axis=0)
    gathered = lax.all_gather(
        lax.all_gather(queries, SEQ[1], axis=0, tiled=True), SEQ[0], axis=0, tiled=True
    )

    def block_partial(block_item):
        q_rows, q_request, q_position = block_item
        row_count = q_rows.shape[0]
        q_four = q_rows.reshape(row_count, kv_heads, head_groups, HD)
        scores = jnp.einsum(
            "bcgd,kcd->bcgk", q_four, key_block, preferred_element_type=jnp.float32
        ) * HD ** (-0.5)
        visible = (q_request[:, None] == key_request[None, :]) & (
            key_position[None, :] <= q_position[:, None]
        )
        visible = visible[:, None, None, :]
        scores = jnp.where(visible, scores, NEGATIVE)
        row_top = jnp.max(scores, axis=-1)
        weights = jnp.where(visible, jnp.exp(scores - row_top[..., None]), 0.0)
        denominator = jnp.sum(weights, axis=-1)
        numerator = jnp.einsum(
            "bcgk,kcd->bcgd",
            weights.astype(jnp.bfloat16),
            value_block,
            preferred_element_type=jnp.float32,
        )
        return (
            row_top.reshape(row_count, q_heads),
            numerator.reshape(row_count, q_heads, HD),
            denominator.reshape(row_count, q_heads),
        )

    def prefill_block(block_item):
        return block_partial(block_item)

    prefill_parts = lax.map(
        prefill_block,
        (
            gathered[:boundary].reshape(PREFILLS, SPAN, q_heads * HD),
            request_all[:boundary].reshape(PREFILLS, SPAN),
            position_all[:boundary].reshape(PREFILLS, SPAN),
        ),
    )
    decode_parts = block_partial(
        (gathered[boundary:], request_all[boundary:], position_all[boundary:])
    )
    row_top = jnp.concatenate(
        [prefill_parts[0].reshape(boundary, q_heads), decode_parts[0]], axis=0
    )
    numerator = jnp.concatenate(
        [prefill_parts[1].reshape(boundary, q_heads, HD), decode_parts[1]], axis=0
    )
    denominator = jnp.concatenate(
        [prefill_parts[2].reshape(boundary, q_heads), decode_parts[2]], axis=0
    )
    part_width = q_heads * (HD + 2)
    packed = jnp.concatenate(
        [numerator, denominator[..., None], row_top[..., None]], axis=-1
    ).reshape(seq_count, tok_rows * part_width)
    received = lax.all_to_all(packed, SEQ, 0, 0, tiled=True).reshape(
        seq_count, tok_rows, q_heads, HD + 2
    )
    part_top = received[..., HD + 1]
    overall = jnp.max(part_top, axis=0)
    factor = jnp.exp(part_top - overall[None])
    numerator = jnp.sum(received[..., :HD] * factor[..., None], axis=0)
    denominator = jnp.sum(received[..., HD] * factor, axis=0)
    attended = (
        (numerator / denominator[..., None]).astype(jnp.bfloat16).reshape(tok_rows, q_heads * HD)
    )
    partial_out = jnp.dot(attended, w_out, preferred_element_type=jnp.float32)
    tp_count = lax.axis_size("tp")
    blocks = partial_out.astype(jnp.bfloat16).reshape(tok_rows, tp_count, -1).transpose(1, 0, 2)
    blocks = lax.all_to_all(blocks, "tp", 0, 0, tiled=True)
    return jnp.sum(blocks.astype(jnp.float32), axis=0).astype(jnp.bfloat16)


def split_mesh(mesh):
    seq_devices = mesh.devices[:, 0]
    try:
        hi = len({d.coords[1] for d in seq_devices})
    except AttributeError:
        hi = 4
    if seq_devices.shape[0] % hi:
        hi = 1
    lo = seq_devices.shape[0] // hi
    grid = mesh.devices.reshape(hi, lo, mesh.devices.shape[1])
    return Mesh(grid, (SEQ[0], SEQ[1], "tp"))


def solution(mesh):
    split = split_mesh(mesh)
    in_specs = (
        P(SEQ, None),
        P(),
        P(None, "tp"),
        P(None, "tp"),
        P(None, "tp"),
        P("tp", None),
        P(SEQ, "tp"),
        P(SEQ, "tp"),
        P(),
        P(SEQ),
    )
    out_specs = P(SEQ, "tp")
    return jax.shard_map(
        per_device, mesh=split, in_specs=in_specs, out_specs=out_specs, check_vma=False
    )
```

```python
import jax
import jax.numpy as jnp
from jax import lax
from jax.sharding import Mesh, PartitionSpec as P

HD = 128
SPAN = 512
PREFILLS = 2


SEQ = ("seq_hi", "seq_lo")
NEGATIVE = -1e30
THETA = 1000000.0
EPSILON = 1e-06


def rotate(values, places):
    half_dim = values.shape[-1] // 2
    frequency = THETA ** (-jnp.arange(half_dim, dtype=jnp.float32) / half_dim)
    angles = places.astype(jnp.float32)[:, None] * frequency[None, :]
    cosine = jnp.cos(angles)[:, None, :]
    sine_part = jnp.sin(angles)[:, None, :]
    front_half = values[..., :half_dim]
    second = values[..., half_dim:]
    return jnp.concatenate(
        [front_half * cosine - second * sine_part, second * cosine + front_half * sine_part],
        axis=-1,
    )


def row_layout(row_count, cached_len):
    position_index = jnp.arange(row_count, dtype=jnp.int32)
    boundary = PREFILLS * SPAN
    request = jnp.where(
        position_index < boundary, position_index // SPAN, PREFILLS + position_index - boundary
    )
    offset = jnp.where(position_index < boundary, position_index % SPAN, 0)
    matches = request[:, None] == jnp.arange(cached_len.shape[0], dtype=jnp.int32)[None, :]
    begins = jnp.sum(jnp.where(matches, cached_len[None, :], 0), axis=1)
    return (request, begins + offset)


def slot_layout(block_number, slot_count, cached_len):
    packed = block_number * slot_count + jnp.arange(slot_count, dtype=jnp.int32)
    ending = jnp.cumsum(cached_len)
    before = packed[:, None] >= ending[None, :]
    request = jnp.sum(before.astype(jnp.int32), axis=1)
    places = packed - jnp.sum(jnp.where(before, cached_len[None, :], 0), axis=1)
    return (request, places)


def per_device(
    tokens,
    norm_gain,
    w_query,
    w_key,
    w_value,
    w_out,
    cache_keys,
    cache_values,
    cached_len,
    block_of_shard,
):
    seq_count = lax.axis_size(SEQ)
    seq_index = lax.axis_index(SEQ)
    tok_rows = tokens.shape[0]
    all_rows = tok_rows * seq_count
    q_heads = w_query.shape[1] // HD
    kv_heads = w_key.shape[1] // HD
    head_groups = q_heads // kv_heads
    boundary = PREFILLS * SPAN
    request_all, position_all = row_layout(all_rows, cached_len)
    my_request = lax.dynamic_slice_in_dim(request_all, seq_index * tok_rows, tok_rows)
    my_position = lax.dynamic_slice_in_dim(position_all, seq_index * tok_rows, tok_rows)
    hidden = tokens.astype(jnp.float32)
    scale_row = lax.rsqrt(jnp.mean(hidden * hidden, axis=1, keepdims=True) + EPSILON)
    normed = (hidden * scale_row * norm_gain.astype(jnp.float32)[None, :]).astype(jnp.bfloat16)
    queries = jnp.dot(normed, w_query, preferred_element_type=jnp.float32).reshape(
        tok_rows, q_heads, HD
    )
    queries = rotate(queries, my_position).astype(jnp.bfloat16).reshape(tok_rows, q_heads * HD)
    new_keys = jnp.dot(normed, w_key, preferred_element_type=jnp.float32).reshape(
        tok_rows, kv_heads, HD
    )
    new_keys = rotate(new_keys, my_position).astype(jnp.bfloat16)
    new_values = (
        jnp.dot(normed, w_value, preferred_element_type=jnp.float32)
        .astype(jnp.bfloat16)
        .reshape(tok_rows, kv_heads, HD)
    )
    key_block = jnp.concatenate([cache_keys.reshape(-1, kv_heads, HD), new_keys], axis=0)
    value_block = jnp.concatenate([cache_values.reshape(-1, kv_heads, HD), new_values], axis=0)
    slot_request, slot_position = slot_layout(block_of_shard[0], cache_keys.shape[0], cached_len)
    key_request = jnp.concatenate([slot_request, my_request], axis=0)
    key_position = jnp.concatenate([slot_position, my_position], axis=0)
    gathered = lax.all_gather(
        lax.all_gather(queries, SEQ[1], axis=0, tiled=True), SEQ[0], axis=0, tiled=True
    )

    def block_partial(block_item):
        q_rows, q_request, q_position = block_item
        row_count = q_rows.shape[0]
        q_four = q_rows.reshape(row_count, kv_heads, head_groups, HD)
        scores = jnp.einsum(
            "bcgd,kcd->bcgk", q_four, key_block, preferred_element_type=jnp.float32
        ) * HD ** (-0.5)
        visible = (q_request[:, None] == key_request[None, :]) & (
            key_position[None, :] <= q_position[:, None]
        )
        visible = visible[:, None, None, :]
        scores = jnp.where(visible, scores, NEGATIVE)
        row_top = jnp.max(scores, axis=-1)
        weights = jnp.where(visible, jnp.exp(scores - row_top[..., None]), 0.0)
        denominator = jnp.sum(weights, axis=-1)
        numerator = jnp.einsum(
            "bcgk,kcd->bcgd",
            weights.astype(jnp.bfloat16),
            value_block,
            preferred_element_type=jnp.float32,
        )
        return (
            row_top.reshape(row_count, q_heads),
            numerator.reshape(row_count, q_heads, HD),
            denominator.reshape(row_count, q_heads),
        )

    def prefill_block(block_item):
        return block_partial(block_item)

    prefill_parts = lax.map(
        prefill_block,
        (
            gathered[:boundary].reshape(PREFILLS, SPAN, q_heads * HD),
            request_all[:boundary].reshape(PREFILLS, SPAN),
            position_all[:boundary].reshape(PREFILLS, SPAN),
        ),
    )
    decode_parts = block_partial(
        (gathered[boundary:], request_all[boundary:], position_all[boundary:])
    )
    row_top = jnp.concatenate(
        [prefill_parts[0].reshape(boundary, q_heads), decode_parts[0]], axis=0
    )
    numerator = jnp.concatenate(
        [prefill_parts[1].reshape(boundary, q_heads, HD), decode_parts[1]], axis=0
    )
    denominator = jnp.concatenate(
        [prefill_parts[2].reshape(boundary, q_heads), decode_parts[2]], axis=0
    )
    pairs = tok_rows * q_heads
    packed = jnp.concatenate(
        [
            numerator.reshape(seq_count, pairs * HD),
            denominator.reshape(seq_count, pairs),
            row_top.reshape(seq_count, pairs),
        ],
        axis=1,
    )
    received = lax.all_to_all(packed, SEQ, 0, 0, tiled=True)
    part_num = received[:, : pairs * HD]
    part_den = received[:, pairs * HD : pairs * (HD + 1)]
    part_top = received[:, pairs * (HD + 1) :]
    overall = jnp.max(part_top, axis=0, keepdims=True)
    factor = jnp.exp(part_top - overall)
    denominator = jnp.sum(part_den * factor, axis=0)
    spread = (
        jnp.arange(pairs, dtype=jnp.int32)[:, None]
        == (jnp.arange(pairs * HD, dtype=jnp.int32) // HD)[None, :]
    ).astype(jnp.float32)
    factor_wide = jnp.dot(factor, spread, precision=lax.Precision.HIGHEST)
    numerator = jnp.sum(part_num * factor_wide, axis=0).reshape(pairs, HD)
    attended = (
        (numerator / denominator[:, None]).astype(jnp.bfloat16).reshape(tok_rows, q_heads * HD)
    )
    partial_out = jnp.dot(attended, w_out, preferred_element_type=jnp.float32)
    tp_count = lax.axis_size("tp")
    blocks = partial_out.astype(jnp.bfloat16).reshape(tok_rows, tp_count, -1).transpose(1, 0, 2)
    blocks = lax.all_to_all(blocks, "tp", 0, 0, tiled=True)
    return jnp.sum(blocks.astype(jnp.float32), axis=0).astype(jnp.bfloat16)


def split_mesh(mesh):
    seq_devices = mesh.devices[:, 0]
    try:
        hi = len({d.coords[1] for d in seq_devices})
    except AttributeError:
        hi = 4
    if seq_devices.shape[0] % hi:
        hi = 1
    lo = seq_devices.shape[0] // hi
    grid = mesh.devices.reshape(hi, lo, mesh.devices.shape[1])
    return Mesh(grid, (SEQ[0], SEQ[1], "tp"))


def solution(mesh):
    split = split_mesh(mesh)
    in_specs = (
        P(SEQ, None),
        P(),
        P(None, "tp"),
        P(None, "tp"),
        P(None, "tp"),
        P("tp", None),
        P(SEQ, "tp"),
        P(SEQ, "tp"),
        P(),
        P(SEQ),
    )
    out_specs = P(SEQ, "tp")
    return jax.shard_map(
        per_device, mesh=split, in_specs=in_specs, out_specs=out_specs, check_vma=False
    )
```

```python
import jax
import jax.numpy as jnp
from jax import lax
from jax.sharding import Mesh, PartitionSpec as P

HD = 128
SPAN = 512
PREFILLS = 2


SEQ = ("seq_hi", "seq_lo")
NEGATIVE = -1e30
THETA = 1000000.0
EPSILON = 1e-06


def rotate(values, places):
    half_dim = values.shape[-1] // 2
    frequency = THETA ** (-jnp.arange(half_dim, dtype=jnp.float32) / half_dim)
    angles = places.astype(jnp.float32)[:, None] * frequency[None, :]
    cosine = jnp.cos(angles)[:, None, :]
    sine_part = jnp.sin(angles)[:, None, :]
    front_half = values[..., :half_dim]
    second = values[..., half_dim:]
    return jnp.concatenate(
        [front_half * cosine - second * sine_part, second * cosine + front_half * sine_part],
        axis=-1,
    )


def row_layout(row_count, cached_len):
    position_index = jnp.arange(row_count, dtype=jnp.int32)
    boundary = PREFILLS * SPAN
    request = jnp.where(
        position_index < boundary, position_index // SPAN, PREFILLS + position_index - boundary
    )
    offset = jnp.where(position_index < boundary, position_index % SPAN, 0)
    matches = request[:, None] == jnp.arange(cached_len.shape[0], dtype=jnp.int32)[None, :]
    begins = jnp.sum(jnp.where(matches, cached_len[None, :], 0), axis=1)
    return (request, begins + offset)


def slot_layout(block_number, slot_count, cached_len):
    packed = block_number * slot_count + jnp.arange(slot_count, dtype=jnp.int32)
    ending = jnp.cumsum(cached_len)
    before = packed[:, None] >= ending[None, :]
    request = jnp.sum(before.astype(jnp.int32), axis=1)
    places = packed - jnp.sum(jnp.where(before, cached_len[None, :], 0), axis=1)
    return (request, places)


def per_device(
    tokens,
    norm_gain,
    w_query,
    w_key,
    w_value,
    w_out,
    cache_keys,
    cache_values,
    cached_len,
    block_of_shard,
):
    seq_count = lax.axis_size(SEQ)
    seq_index = lax.axis_index(SEQ)
    tok_rows = tokens.shape[0]
    all_rows = tok_rows * seq_count
    q_heads = w_query.shape[1] // HD
    kv_heads = w_key.shape[1] // HD
    head_groups = q_heads // kv_heads
    boundary = PREFILLS * SPAN
    request_all, position_all = row_layout(all_rows, cached_len)
    my_request = lax.dynamic_slice_in_dim(request_all, seq_index * tok_rows, tok_rows)
    my_position = lax.dynamic_slice_in_dim(position_all, seq_index * tok_rows, tok_rows)
    hidden = tokens.astype(jnp.float32)
    scale_row = lax.rsqrt(jnp.mean(hidden * hidden, axis=1, keepdims=True) + EPSILON)
    normed = (hidden * scale_row * norm_gain.astype(jnp.float32)[None, :]).astype(jnp.bfloat16)
    queries = jnp.dot(normed, w_query, preferred_element_type=jnp.float32).reshape(
        tok_rows, q_heads, HD
    )
    queries = rotate(queries, my_position).astype(jnp.bfloat16).reshape(tok_rows, q_heads * HD)
    new_keys = jnp.dot(normed, w_key, preferred_element_type=jnp.float32).reshape(
        tok_rows, kv_heads, HD
    )
    new_keys = rotate(new_keys, my_position).astype(jnp.bfloat16)
    new_values = (
        jnp.dot(normed, w_value, preferred_element_type=jnp.float32)
        .astype(jnp.bfloat16)
        .reshape(tok_rows, kv_heads, HD)
    )
    key_block = jnp.concatenate([cache_keys.reshape(-1, kv_heads, HD), new_keys], axis=0)
    value_block = jnp.concatenate([cache_values.reshape(-1, kv_heads, HD), new_values], axis=0)
    slot_request, slot_position = slot_layout(block_of_shard[0], cache_keys.shape[0], cached_len)
    key_request = jnp.concatenate([slot_request, my_request], axis=0)
    key_position = jnp.concatenate([slot_position, my_position], axis=0)
    gathered = lax.all_gather(
        lax.all_gather(queries, SEQ[1], axis=0, tiled=True), SEQ[0], axis=0, tiled=True
    )

    def block_partial(block_item):
        q_rows, q_request, q_position = block_item
        row_count = q_rows.shape[0]
        q_four = q_rows.reshape(row_count, kv_heads, head_groups, HD)
        scores = jnp.einsum(
            "bcgd,kcd->bcgk", q_four, key_block, preferred_element_type=jnp.float32
        ) * HD ** (-0.5)
        visible = (q_request[:, None] == key_request[None, :]) & (
            key_position[None, :] <= q_position[:, None]
        )
        visible = visible[:, None, None, :]
        scores = jnp.where(visible, scores, NEGATIVE)
        row_top = jnp.max(scores, axis=-1)
        weights = jnp.where(visible, jnp.exp(scores - row_top[..., None]), 0.0)
        denominator = jnp.sum(weights, axis=-1)
        numerator = jnp.einsum(
            "bcgk,kcd->bcgd",
            weights.astype(jnp.bfloat16),
            value_block,
            preferred_element_type=jnp.float32,
        )
        return (
            row_top.reshape(row_count, q_heads),
            numerator.reshape(row_count, q_heads, HD),
            denominator.reshape(row_count, q_heads),
        )

    def prefill_block(block_item):
        return block_partial(block_item)

    prefill_parts = lax.map(
        prefill_block,
        (
            gathered[:boundary].reshape(PREFILLS, SPAN, q_heads * HD),
            request_all[:boundary].reshape(PREFILLS, SPAN),
            position_all[:boundary].reshape(PREFILLS, SPAN),
        ),
    )
    decode_parts = block_partial(
        (gathered[boundary:], request_all[boundary:], position_all[boundary:])
    )
    row_top = jnp.concatenate(
        [prefill_parts[0].reshape(boundary, q_heads), decode_parts[0]], axis=0
    )
    numerator = jnp.concatenate(
        [prefill_parts[1].reshape(boundary, q_heads, HD), decode_parts[1]], axis=0
    )
    denominator = jnp.concatenate(
        [prefill_parts[2].reshape(boundary, q_heads), decode_parts[2]], axis=0
    )
    pairs = tok_rows * q_heads
    seen = denominator > 0
    average = numerator / jnp.maximum(denominator, 1.0)[..., None]
    log_weight = jnp.where(seen, row_top + jnp.log(jnp.where(seen, denominator, 1.0)), NEGATIVE)
    high = lax.reduce_precision(log_weight, exponent_bits=8, mantissa_bits=7)
    rest = log_weight - high
    middle = lax.reduce_precision(rest, exponent_bits=8, mantissa_bits=7)
    low = rest - middle
    packed = jnp.concatenate(
        [
            average.astype(jnp.bfloat16).reshape(seq_count, pairs * HD),
            high.astype(jnp.bfloat16).reshape(seq_count, pairs),
            middle.astype(jnp.bfloat16).reshape(seq_count, pairs),
            low.astype(jnp.bfloat16).reshape(seq_count, pairs),
        ],
        axis=1,
    )
    received = lax.all_to_all(packed, SEQ, 0, 0, tiled=True)
    part_avg = received[:, : pairs * HD].astype(jnp.float32)
    tail = received[:, pairs * HD :].astype(jnp.float32).reshape(seq_count, 3, pairs)
    part_log = tail[:, 0] + (tail[:, 1] + tail[:, 2])
    overall = jnp.max(part_log, axis=0, keepdims=True)
    factor = jnp.exp(part_log - overall)
    denominator = jnp.sum(factor, axis=0)
    spread = (
        jnp.arange(pairs, dtype=jnp.int32)[:, None]
        == (jnp.arange(pairs * HD, dtype=jnp.int32) // HD)[None, :]
    ).astype(jnp.float32)
    factor_wide = jnp.dot(factor, spread, precision=lax.Precision.HIGHEST)
    numerator = jnp.sum(part_avg * factor_wide, axis=0).reshape(pairs, HD)
    attended = (
        (numerator / denominator[:, None]).astype(jnp.bfloat16).reshape(tok_rows, q_heads * HD)
    )
    partial_out = jnp.dot(attended, w_out, preferred_element_type=jnp.float32)
    tp_count = lax.axis_size("tp")
    blocks = partial_out.astype(jnp.bfloat16).reshape(tok_rows, tp_count, -1).transpose(1, 0, 2)
    blocks = lax.all_to_all(blocks, "tp", 0, 0, tiled=True)
    return jnp.sum(blocks.astype(jnp.float32), axis=0).astype(jnp.bfloat16)


def split_mesh(mesh):
    seq_devices = mesh.devices[:, 0]
    try:
        hi = len({d.coords[1] for d in seq_devices})
    except AttributeError:
        hi = 4
    if seq_devices.shape[0] % hi:
        hi = 1
    lo = seq_devices.shape[0] // hi
    grid = mesh.devices.reshape(hi, lo, mesh.devices.shape[1])
    return Mesh(grid, (SEQ[0], SEQ[1], "tp"))


def solution(mesh):
    split = split_mesh(mesh)
    in_specs = (
        P(SEQ, None),
        P(),
        P(None, "tp"),
        P(None, "tp"),
        P(None, "tp"),
        P("tp", None),
        P(SEQ, "tp"),
        P(SEQ, "tp"),
        P(),
        P(SEQ),
    )
    out_specs = P(SEQ, "tp")
    return jax.shard_map(
        per_device, mesh=split, in_specs=in_specs, out_specs=out_specs, check_vma=False
    )
```

```python
import functools

import jax
import jax.numpy as jnp
from jax import lax
from jax.experimental import pallas as pl
from jax.sharding import Mesh, PartitionSpec as P

HD = 128
SPAN = 512
PREFILLS = 2


SEQ = ("seq_hi", "seq_lo")
NEGATIVE = -1e30
THETA = 1000000.0
EPSILON = 1e-06


def rotate(values, places):
    half_dim = values.shape[-1] // 2
    frequency = THETA ** (-jnp.arange(half_dim, dtype=jnp.float32) / half_dim)
    angles = places.astype(jnp.float32)[:, None] * frequency[None, :]
    cosine = jnp.cos(angles)[:, None, :]
    sine_part = jnp.sin(angles)[:, None, :]
    front_half = values[..., :half_dim]
    second = values[..., half_dim:]
    return jnp.concatenate(
        [front_half * cosine - second * sine_part, second * cosine + front_half * sine_part],
        axis=-1,
    )


def row_layout(row_count, cached_len):
    position_index = jnp.arange(row_count, dtype=jnp.int32)
    boundary = PREFILLS * SPAN
    request = jnp.where(
        position_index < boundary, position_index // SPAN, PREFILLS + position_index - boundary
    )
    offset = jnp.where(position_index < boundary, position_index % SPAN, 0)
    matches = request[:, None] == jnp.arange(cached_len.shape[0], dtype=jnp.int32)[None, :]
    begins = jnp.sum(jnp.where(matches, cached_len[None, :], 0), axis=1)
    return (request, begins + offset)


def slot_layout(block_number, slot_count, cached_len):
    packed = block_number * slot_count + jnp.arange(slot_count, dtype=jnp.int32)
    ending = jnp.cumsum(cached_len)
    before = packed[:, None] >= ending[None, :]
    request = jnp.sum(before.astype(jnp.int32), axis=1)
    places = packed - jnp.sum(jnp.where(before, cached_len[None, :], 0), axis=1)
    return (request, places)


def attend_kernel(
    q_ref, qr_ref, qp_ref, k_ref, v_ref, kr_ref, kp_ref, nk_ref, nv_ref, nr_ref, np_ref,
    avg_ref, lw_ref, *, heads
):
    seen_cache = (qr_ref[...] == kr_ref[...]) & (kp_ref[...] <= qp_ref[...])
    seen_new = (qr_ref[...] == nr_ref[...]) & (np_ref[...] <= qp_ref[...])
    tops = []
    for g in range(heads):
        qg = q_ref[:, g * HD:(g + 1) * HD]
        dims = (((1,), (1,)), ((), ()))
        cache_scores = lax.dot_general(
            qg, k_ref[...], dims, preferred_element_type=jnp.float32
        ) * HD ** (-0.5)
        new_scores = lax.dot_general(
            qg, nk_ref[...], dims, preferred_element_type=jnp.float32
        ) * HD ** (-0.5)
        cache_scores = jnp.where(seen_cache, cache_scores, NEGATIVE)
        new_scores = jnp.where(seen_new, new_scores, NEGATIVE)
        top = jnp.maximum(
            jnp.max(cache_scores, axis=1, keepdims=True), jnp.max(new_scores, axis=1, keepdims=True)
        )
        cache_weights = jnp.exp(cache_scores - top)
        new_weights = jnp.exp(new_scores - top)
        den = jnp.sum(cache_weights, axis=1, keepdims=True) + jnp.sum(
            new_weights, axis=1, keepdims=True
        )
        num = jnp.dot(
            cache_weights.astype(jnp.bfloat16), v_ref[...], preferred_element_type=jnp.float32
        ) + jnp.dot(new_weights.astype(jnp.bfloat16), nv_ref[...], preferred_element_type=jnp.float32)
        some = top > 0.5 * NEGATIVE
        avg_ref[:, g * HD:(g + 1) * HD] = jnp.where(some, num / den, 0.0).astype(avg_ref.dtype)
        tops.append(jnp.where(some, top + jnp.log(den), NEGATIVE))
    lw_ref[...] = jnp.concatenate(tops, axis=1)


def attend(q, q_req, q_pos, keys, values, k_req, k_pos, new_k, new_v, n_req, n_pos, block_rows=136):
    rows, width = q.shape
    heads = width // HD
    slots = keys.shape[0]
    fresh = new_k.shape[0]
    grid = (rows // block_rows,)
    row_block = lambda i: (i, 0)
    whole = lambda i: (0, 0)
    return pl.pallas_call(
        functools.partial(attend_kernel, heads=heads),
        grid=grid,
        in_specs=[
            pl.BlockSpec((block_rows, width), row_block),
            pl.BlockSpec((block_rows, 1), row_block),
            pl.BlockSpec((block_rows, 1), row_block),
            pl.BlockSpec((slots, HD), whole),
            pl.BlockSpec((slots, HD), whole),
            pl.BlockSpec((1, slots), whole),
            pl.BlockSpec((1, slots), whole),
            pl.BlockSpec((fresh, HD), whole),
            pl.BlockSpec((fresh, HD), whole),
            pl.BlockSpec((1, fresh), whole),
            pl.BlockSpec((1, fresh), whole),
        ],
        out_specs=[
            pl.BlockSpec((block_rows, width), row_block),
            pl.BlockSpec((block_rows, heads), row_block),
        ],
        out_shape=[
            jax.ShapeDtypeStruct((rows, width), jnp.bfloat16),
            jax.ShapeDtypeStruct((rows, heads), jnp.float32),
        ],
    )(
        q, q_req.reshape(rows, 1), q_pos.reshape(rows, 1), keys, values,
        k_req.reshape(1, slots), k_pos.reshape(1, slots),
        new_k, new_v, n_req.reshape(1, fresh), n_pos.reshape(1, fresh),
    )


def per_device(
    tokens,
    norm_gain,
    w_query,
    w_key,
    w_value,
    w_out,
    cache_keys,
    cache_values,
    cached_len,
    block_of_shard,
):
    seq_count = lax.axis_size(SEQ)
    seq_index = lax.axis_index(SEQ)
    tok_rows = tokens.shape[0]
    all_rows = tok_rows * seq_count
    q_heads = w_query.shape[1] // HD
    kv_heads = w_key.shape[1] // HD
    head_groups = q_heads // kv_heads
    boundary = PREFILLS * SPAN
    request_all, position_all = row_layout(all_rows, cached_len)
    my_request = lax.dynamic_slice_in_dim(request_all, seq_index * tok_rows, tok_rows)
    my_position = lax.dynamic_slice_in_dim(position_all, seq_index * tok_rows, tok_rows)
    hidden = tokens.astype(jnp.float32)
    scale_row = lax.rsqrt(jnp.mean(hidden * hidden, axis=1, keepdims=True) + EPSILON)
    normed = (hidden * scale_row * norm_gain.astype(jnp.float32)[None, :]).astype(jnp.bfloat16)
    queries = jnp.dot(normed, w_query, preferred_element_type=jnp.float32).reshape(
        tok_rows, q_heads, HD
    )
    queries = rotate(queries, my_position).astype(jnp.bfloat16).reshape(tok_rows, q_heads * HD)
    new_keys = jnp.dot(normed, w_key, preferred_element_type=jnp.float32).reshape(
        tok_rows, kv_heads, HD
    )
    new_keys = rotate(new_keys, my_position).astype(jnp.bfloat16)
    new_values = (
        jnp.dot(normed, w_value, preferred_element_type=jnp.float32)
        .astype(jnp.bfloat16)
        .reshape(tok_rows, kv_heads, HD)
    )
    extra = -(-tok_rows // 128) * 128 - tok_rows
    new_k = jnp.concatenate(
        [new_keys.reshape(tok_rows, HD), jnp.zeros((extra, HD), jnp.bfloat16)], axis=0
    )
    new_v = jnp.concatenate(
        [new_values.reshape(tok_rows, HD), jnp.zeros((extra, HD), jnp.bfloat16)], axis=0
    )
    new_req = jnp.concatenate([my_request, jnp.full((extra,), -1, jnp.int32)], axis=0)
    new_pos = jnp.concatenate([my_position, jnp.zeros((extra,), jnp.int32)], axis=0)
    slot_request, slot_position = slot_layout(block_of_shard[0], cache_keys.shape[0], cached_len)
    gathered = lax.all_gather(
        lax.all_gather(queries, SEQ[1], axis=0, tiled=True), SEQ[0], axis=0, tiled=True
    )
    average, log_weight = attend(
        gathered, request_all, position_all, cache_keys, cache_values, slot_request, slot_position,
        new_k, new_v, new_req, new_pos,
    )
    pairs = tok_rows * q_heads
    high = lax.reduce_precision(log_weight, exponent_bits=8, mantissa_bits=7)
    rest = log_weight - high
    middle = lax.reduce_precision(rest, exponent_bits=8, mantissa_bits=7)
    low = rest - middle
    packed = jnp.concatenate(
        [
            average.astype(jnp.bfloat16).reshape(seq_count, pairs * HD),
            high.astype(jnp.bfloat16).reshape(seq_count, pairs),
            middle.astype(jnp.bfloat16).reshape(seq_count, pairs),
            low.astype(jnp.bfloat16).reshape(seq_count, pairs),
        ],
        axis=1,
    )
    received = lax.all_to_all(packed, SEQ, 0, 0, tiled=True)
    part_avg = received[:, : pairs * HD].astype(jnp.float32)
    tail = received[:, pairs * HD :].astype(jnp.float32).reshape(seq_count, 3, pairs)
    part_log = tail[:, 0] + (tail[:, 1] + tail[:, 2])
    overall = jnp.max(part_log, axis=0, keepdims=True)
    factor = jnp.exp(part_log - overall)
    denominator = jnp.sum(factor, axis=0)
    spread = (
        jnp.arange(pairs, dtype=jnp.int32)[:, None]
        == (jnp.arange(pairs * HD, dtype=jnp.int32) // HD)[None, :]
    ).astype(jnp.float32)
    factor_wide = jnp.dot(factor, spread, precision=lax.Precision.HIGHEST)
    numerator = jnp.sum(part_avg * factor_wide, axis=0).reshape(pairs, HD)
    attended = (
        (numerator / denominator[:, None]).astype(jnp.bfloat16).reshape(tok_rows, q_heads * HD)
    )
    partial_out = jnp.dot(attended, w_out, preferred_element_type=jnp.float32)
    tp_count = lax.axis_size("tp")
    blocks = partial_out.astype(jnp.bfloat16).reshape(tok_rows, tp_count, -1).transpose(1, 0, 2)
    blocks = lax.all_to_all(blocks, "tp", 0, 0, tiled=True)
    return jnp.sum(blocks.astype(jnp.float32), axis=0).astype(jnp.bfloat16)


def split_mesh(mesh):
    seq_devices = mesh.devices[:, 0]
    try:
        hi = len({d.coords[1] for d in seq_devices})
    except AttributeError:
        hi = 4
    if seq_devices.shape[0] % hi:
        hi = 1
    lo = seq_devices.shape[0] // hi
    grid = mesh.devices.reshape(hi, lo, mesh.devices.shape[1])
    return Mesh(grid, (SEQ[0], SEQ[1], "tp"))


def solution(mesh):
    split = split_mesh(mesh)
    in_specs = (
        P(SEQ, None),
        P(),
        P(None, "tp"),
        P(None, "tp"),
        P(None, "tp"),
        P("tp", None),
        P(SEQ, "tp"),
        P(SEQ, "tp"),
        P(),
        P(SEQ),
    )
    out_specs = P(SEQ, "tp")
    return jax.shard_map(
        per_device, mesh=split, in_specs=in_specs, out_specs=out_specs, check_vma=False
    )
```

```python
import functools

import jax
import jax.numpy as jnp
from jax import lax
from jax.experimental import pallas as pl
from jax.sharding import Mesh, PartitionSpec as P

HD = 128
SPAN = 512
PREFILLS = 2


SEQ = ("seq_hi", "seq_lo")
NEGATIVE = -1e30
THETA = 1000000.0
EPSILON = 1e-06


def rotate(values, places):
    half_dim = values.shape[-1] // 2
    frequency = THETA ** (-jnp.arange(half_dim, dtype=jnp.float32) / half_dim)
    angles = places.astype(jnp.float32)[:, None] * frequency[None, :]
    cosine = jnp.cos(angles)[:, None, :]
    sine_part = jnp.sin(angles)[:, None, :]
    front_half = values[..., :half_dim]
    second = values[..., half_dim:]
    return jnp.concatenate(
        [front_half * cosine - second * sine_part, second * cosine + front_half * sine_part],
        axis=-1,
    )


def row_layout(row_count, cached_len):
    position_index = jnp.arange(row_count, dtype=jnp.int32)
    boundary = PREFILLS * SPAN
    request = jnp.where(
        position_index < boundary, position_index // SPAN, PREFILLS + position_index - boundary
    )
    offset = jnp.where(position_index < boundary, position_index % SPAN, 0)
    matches = request[:, None] == jnp.arange(cached_len.shape[0], dtype=jnp.int32)[None, :]
    begins = jnp.sum(jnp.where(matches, cached_len[None, :], 0), axis=1)
    return (request, begins + offset)


def slot_layout(block_number, slot_count, cached_len):
    packed = block_number * slot_count + jnp.arange(slot_count, dtype=jnp.int32)
    ending = jnp.cumsum(cached_len)
    before = packed[:, None] >= ending[None, :]
    request = jnp.sum(before.astype(jnp.int32), axis=1)
    places = packed - jnp.sum(jnp.where(before, cached_len[None, :], 0), axis=1)
    return (request, places)


def attend_kernel(
    q_ref, qr_ref, qp_ref, k_ref, v_ref, kr_ref, kp_ref, nk_ref, nv_ref, nr_ref, np_ref,
    avg_ref, lw_ref, *, heads
):
    seen_cache = qr_ref[...] == kr_ref[...]
    seen_new = (qr_ref[...] == nr_ref[...]) & (np_ref[...] <= qp_ref[...])
    tops = []
    for g in range(heads):
        qg = q_ref[:, g * HD:(g + 1) * HD]
        dims = (((1,), (1,)), ((), ()))
        cache_scores = lax.dot_general(
            qg, k_ref[...], dims, preferred_element_type=jnp.float32
        ) * HD ** (-0.5)
        new_scores = lax.dot_general(
            qg, nk_ref[...], dims, preferred_element_type=jnp.float32
        ) * HD ** (-0.5)
        cache_scores = jnp.where(seen_cache, cache_scores, NEGATIVE)
        new_scores = jnp.where(seen_new, new_scores, NEGATIVE)
        top = jnp.maximum(
            jnp.max(cache_scores, axis=1, keepdims=True), jnp.max(new_scores, axis=1, keepdims=True)
        )
        cache_weights = jnp.exp(cache_scores - top)
        new_weights = jnp.exp(new_scores - top)
        den = jnp.sum(cache_weights, axis=1, keepdims=True) + jnp.sum(
            new_weights, axis=1, keepdims=True
        )
        num = jnp.dot(
            cache_weights.astype(jnp.bfloat16), v_ref[...], preferred_element_type=jnp.float32
        ) + jnp.dot(new_weights.astype(jnp.bfloat16), nv_ref[...], preferred_element_type=jnp.float32)
        some = top > 0.5 * NEGATIVE
        avg_ref[:, g * HD:(g + 1) * HD] = jnp.where(some, num / den, 0.0).astype(avg_ref.dtype)
        tops.append(jnp.where(some, top + jnp.log(den), NEGATIVE))
    lw_ref[...] = jnp.concatenate(tops, axis=1)


def attend(q, q_req, q_pos, keys, values, k_req, k_pos, new_k, new_v, n_req, n_pos, block_rows=136):
    rows, width = q.shape
    heads = width // HD
    slots = keys.shape[0]
    fresh = new_k.shape[0]
    grid = (rows // block_rows,)
    row_block = lambda i: (i, 0)
    whole = lambda i: (0, 0)
    return pl.pallas_call(
        functools.partial(attend_kernel, heads=heads),
        grid=grid,
        in_specs=[
            pl.BlockSpec((block_rows, width), row_block),
            pl.BlockSpec((block_rows, 1), row_block),
            pl.BlockSpec((block_rows, 1), row_block),
            pl.BlockSpec((slots, HD), whole),
            pl.BlockSpec((slots, HD), whole),
            pl.BlockSpec((1, slots), whole),
            pl.BlockSpec((1, slots), whole),
            pl.BlockSpec((fresh, HD), whole),
            pl.BlockSpec((fresh, HD), whole),
            pl.BlockSpec((1, fresh), whole),
            pl.BlockSpec((1, fresh), whole),
        ],
        out_specs=[
            pl.BlockSpec((block_rows, width), row_block),
            pl.BlockSpec((block_rows, heads), row_block),
        ],
        out_shape=[
            jax.ShapeDtypeStruct((rows, width), jnp.bfloat16),
            jax.ShapeDtypeStruct((rows, heads), jnp.float32),
        ],
    )(
        q, q_req.reshape(rows, 1), q_pos.reshape(rows, 1), keys, values,
        k_req.reshape(1, slots), k_pos.reshape(1, slots),
        new_k, new_v, n_req.reshape(1, fresh), n_pos.reshape(1, fresh),
    )


def per_device(
    tokens,
    norm_gain,
    w_query,
    w_key,
    w_value,
    w_out,
    cache_keys,
    cache_values,
    cached_len,
    block_of_shard,
):
    seq_count = lax.axis_size(SEQ)
    seq_index = lax.axis_index(SEQ)
    tok_rows = tokens.shape[0]
    all_rows = tok_rows * seq_count
    q_heads = w_query.shape[1] // HD
    kv_heads = w_key.shape[1] // HD
    head_groups = q_heads // kv_heads
    boundary = PREFILLS * SPAN
    request_all, position_all = row_layout(all_rows, cached_len)
    my_request = lax.dynamic_slice_in_dim(request_all, seq_index * tok_rows, tok_rows)
    my_position = lax.dynamic_slice_in_dim(position_all, seq_index * tok_rows, tok_rows)
    hidden = tokens.astype(jnp.float32)
    scale_row = lax.rsqrt(jnp.mean(hidden * hidden, axis=1, keepdims=True) + EPSILON)
    normed = (hidden * scale_row * norm_gain.astype(jnp.float32)[None, :]).astype(jnp.bfloat16)
    queries = jnp.dot(normed, w_query, preferred_element_type=jnp.float32).reshape(
        tok_rows, q_heads, HD
    )
    queries = rotate(queries, my_position).astype(jnp.bfloat16).reshape(tok_rows, q_heads * HD)
    new_keys = jnp.dot(normed, w_key, preferred_element_type=jnp.float32).reshape(
        tok_rows, kv_heads, HD
    )
    new_keys = rotate(new_keys, my_position).astype(jnp.bfloat16)
    new_values = (
        jnp.dot(normed, w_value, preferred_element_type=jnp.float32)
        .astype(jnp.bfloat16)
        .reshape(tok_rows, kv_heads, HD)
    )
    extra = -(-tok_rows // 128) * 128 - tok_rows
    new_k = jnp.concatenate(
        [new_keys.reshape(tok_rows, HD), jnp.zeros((extra, HD), jnp.bfloat16)], axis=0
    )
    new_v = jnp.concatenate(
        [new_values.reshape(tok_rows, HD), jnp.zeros((extra, HD), jnp.bfloat16)], axis=0
    )
    new_req = jnp.concatenate([my_request, jnp.full((extra,), -1, jnp.int32)], axis=0)
    new_pos = jnp.concatenate([my_position, jnp.zeros((extra,), jnp.int32)], axis=0)
    slot_request, slot_position = slot_layout(block_of_shard[0], cache_keys.shape[0], cached_len)
    gathered = lax.all_gather(
        lax.all_gather(queries, SEQ[1], axis=0, tiled=True), SEQ[0], axis=0, tiled=True
    )
    average, log_weight = attend(
        gathered, request_all, position_all, cache_keys, cache_values, slot_request, slot_position,
        new_k, new_v, new_req, new_pos,
    )
    pairs = tok_rows * q_heads
    high = lax.reduce_precision(log_weight, exponent_bits=8, mantissa_bits=7)
    rest = log_weight - high
    middle = lax.reduce_precision(rest, exponent_bits=8, mantissa_bits=7)
    low = rest - middle
    packed = jnp.concatenate(
        [
            average.astype(jnp.bfloat16).reshape(seq_count, pairs * HD),
            high.astype(jnp.bfloat16).reshape(seq_count, pairs),
            middle.astype(jnp.bfloat16).reshape(seq_count, pairs),
            low.astype(jnp.bfloat16).reshape(seq_count, pairs),
        ],
        axis=1,
    )
    received = lax.all_to_all(packed, SEQ, 0, 0, tiled=True)
    part_avg = received[:, : pairs * HD].astype(jnp.float32)
    tail = received[:, pairs * HD :].astype(jnp.float32).reshape(seq_count, 3, pairs)
    part_log = tail[:, 0] + (tail[:, 1] + tail[:, 2])
    overall = jnp.max(part_log, axis=0, keepdims=True)
    factor = jnp.exp(part_log - overall)
    denominator = jnp.sum(factor, axis=0)
    spread = (
        jnp.arange(pairs, dtype=jnp.int32)[:, None]
        == (jnp.arange(pairs * HD, dtype=jnp.int32) // HD)[None, :]
    ).astype(jnp.float32)
    factor_wide = jnp.dot(factor, spread, precision=lax.Precision.HIGHEST)
    numerator = jnp.sum(part_avg * factor_wide, axis=0).reshape(pairs, HD)
    attended = (
        (numerator / denominator[:, None]).astype(jnp.bfloat16).reshape(tok_rows, q_heads * HD)
    )
    partial_out = jnp.dot(attended, w_out, preferred_element_type=jnp.float32)
    tp_count = lax.axis_size("tp")
    blocks = partial_out.astype(jnp.bfloat16).reshape(tok_rows, tp_count, -1).transpose(1, 0, 2)
    blocks = lax.all_to_all(blocks, "tp", 0, 0, tiled=True)
    return jnp.sum(blocks.astype(jnp.float32), axis=0).astype(jnp.bfloat16)


def split_mesh(mesh):
    seq_devices = mesh.devices[:, 0]
    try:
        hi = len({d.coords[1] for d in seq_devices})
    except AttributeError:
        hi = 4
    if seq_devices.shape[0] % hi:
        hi = 1
    lo = seq_devices.shape[0] // hi
    grid = mesh.devices.reshape(hi, lo, mesh.devices.shape[1])
    return Mesh(grid, (SEQ[0], SEQ[1], "tp"))


def solution(mesh):
    split = split_mesh(mesh)
    in_specs = (
        P(SEQ, None),
        P(),
        P(None, "tp"),
        P(None, "tp"),
        P(None, "tp"),
        P("tp", None),
        P(SEQ, "tp"),
        P(SEQ, "tp"),
        P(),
        P(SEQ),
    )
    out_specs = P(SEQ, "tp")
    return jax.shard_map(
        per_device, mesh=split, in_specs=in_specs, out_specs=out_specs, check_vma=False
    )
```

```python
import functools

import jax
import jax.numpy as jnp
from jax import lax
from jax.experimental import pallas as pl
from jax.sharding import Mesh, PartitionSpec as P

HD = 128
SPAN = 512
PREFILLS = 2


SEQ = ("seq_hi", "seq_lo")
NEGATIVE = -1e30
THETA = 1000000.0
EPSILON = 1e-06


def rotate(values, places):
    half_dim = values.shape[-1] // 2
    frequency = THETA ** (-jnp.arange(half_dim, dtype=jnp.float32) / half_dim)
    angles = places.astype(jnp.float32)[:, None] * frequency[None, :]
    cosine = jnp.cos(angles)[:, None, :]
    sine_part = jnp.sin(angles)[:, None, :]
    front_half = values[..., :half_dim]
    second = values[..., half_dim:]
    return jnp.concatenate(
        [front_half * cosine - second * sine_part, second * cosine + front_half * sine_part],
        axis=-1,
    )


def row_layout(row_count, cached_len):
    position_index = jnp.arange(row_count, dtype=jnp.int32)
    boundary = PREFILLS * SPAN
    request = jnp.where(
        position_index < boundary, position_index // SPAN, PREFILLS + position_index - boundary
    )
    offset = jnp.where(position_index < boundary, position_index % SPAN, 0)
    matches = request[:, None] == jnp.arange(cached_len.shape[0], dtype=jnp.int32)[None, :]
    begins = jnp.sum(jnp.where(matches, cached_len[None, :], 0), axis=1)
    return (request, begins + offset)


def slot_layout(block_number, slot_count, cached_len):
    packed = block_number * slot_count + jnp.arange(slot_count, dtype=jnp.int32)
    ending = jnp.cumsum(cached_len)
    before = packed[:, None] >= ending[None, :]
    request = jnp.sum(before.astype(jnp.int32), axis=1)
    places = packed - jnp.sum(jnp.where(before, cached_len[None, :], 0), axis=1)
    return (request, places)


def attend_kernel(
    q_ref, qr_ref, qp_ref, k_ref, v_ref, kr_ref, kp_ref, nk_ref, nv_ref, nr_ref, np_ref,
    avg_ref, lw_ref, *, heads
):
    seen_cache = qr_ref[...] == kr_ref[...]
    seen_new = (qr_ref[...] == nr_ref[...]) & (np_ref[...] <= qp_ref[...])
    tops = []
    for g in range(heads):
        qg = q_ref[:, g * HD:(g + 1) * HD]
        dims = (((1,), (1,)), ((), ()))
        cache_scores = lax.dot_general(
            qg, k_ref[...], dims, preferred_element_type=jnp.float32
        ) * HD ** (-0.5)
        new_scores = lax.dot_general(
            qg, nk_ref[...], dims, preferred_element_type=jnp.float32
        ) * HD ** (-0.5)
        cache_scores = jnp.where(seen_cache, cache_scores, NEGATIVE)
        new_scores = jnp.where(seen_new, new_scores, NEGATIVE)
        top = jnp.maximum(
            jnp.max(cache_scores, axis=1, keepdims=True), jnp.max(new_scores, axis=1, keepdims=True)
        )
        cache_weights = jnp.exp(cache_scores - top)
        new_weights = jnp.exp(new_scores - top)
        den = jnp.sum(cache_weights, axis=1, keepdims=True) + jnp.sum(
            new_weights, axis=1, keepdims=True
        )
        num = jnp.dot(
            cache_weights.astype(jnp.bfloat16), v_ref[...], preferred_element_type=jnp.float32
        ) + jnp.dot(new_weights.astype(jnp.bfloat16), nv_ref[...], preferred_element_type=jnp.float32)
        some = top > 0.5 * NEGATIVE
        avg_ref[:, g * HD:(g + 1) * HD] = jnp.where(some, num / den, 0.0).astype(avg_ref.dtype)
        tops.append(jnp.where(some, top + jnp.log(den), NEGATIVE))
    lw_ref[...] = jnp.concatenate(tops, axis=1)


def attend(q, q_req, q_pos, keys, values, k_req, k_pos, new_k, new_v, n_req, n_pos, block_rows=272):
    rows, width = q.shape
    heads = width // HD
    slots = keys.shape[0]
    fresh = new_k.shape[0]
    grid = (rows // block_rows,)
    row_block = lambda i: (i, 0)
    whole = lambda i: (0, 0)
    return pl.pallas_call(
        functools.partial(attend_kernel, heads=heads),
        grid=grid,
        in_specs=[
            pl.BlockSpec((block_rows, width), row_block),
            pl.BlockSpec((block_rows, 1), row_block),
            pl.BlockSpec((block_rows, 1), row_block),
            pl.BlockSpec((slots, HD), whole),
            pl.BlockSpec((slots, HD), whole),
            pl.BlockSpec((1, slots), whole),
            pl.BlockSpec((1, slots), whole),
            pl.BlockSpec((fresh, HD), whole),
            pl.BlockSpec((fresh, HD), whole),
            pl.BlockSpec((1, fresh), whole),
            pl.BlockSpec((1, fresh), whole),
        ],
        out_specs=[
            pl.BlockSpec((block_rows, width), row_block),
            pl.BlockSpec((block_rows, heads), row_block),
        ],
        out_shape=[
            jax.ShapeDtypeStruct((rows, width), jnp.bfloat16),
            jax.ShapeDtypeStruct((rows, heads), jnp.float32),
        ],
    )(
        q, q_req.reshape(rows, 1), q_pos.reshape(rows, 1), keys, values,
        k_req.reshape(1, slots), k_pos.reshape(1, slots),
        new_k, new_v, n_req.reshape(1, fresh), n_pos.reshape(1, fresh),
    )


def per_device(
    tokens,
    norm_gain,
    w_query,
    w_key,
    w_value,
    w_out,
    cache_keys,
    cache_values,
    cached_len,
    block_of_shard,
):
    seq_count = lax.axis_size(SEQ)
    seq_index = lax.axis_index(SEQ)
    tok_rows = tokens.shape[0]
    all_rows = tok_rows * seq_count
    q_heads = w_query.shape[1] // HD
    kv_heads = w_key.shape[1] // HD
    head_groups = q_heads // kv_heads
    boundary = PREFILLS * SPAN
    request_all, position_all = row_layout(all_rows, cached_len)
    my_request = lax.dynamic_slice_in_dim(request_all, seq_index * tok_rows, tok_rows)
    my_position = lax.dynamic_slice_in_dim(position_all, seq_index * tok_rows, tok_rows)
    hidden = tokens.astype(jnp.float32)
    scale_row = lax.rsqrt(jnp.mean(hidden * hidden, axis=1, keepdims=True) + EPSILON)
    normed = (hidden * scale_row * norm_gain.astype(jnp.float32)[None, :]).astype(jnp.bfloat16)
    queries = jnp.dot(normed, w_query, preferred_element_type=jnp.float32).reshape(
        tok_rows, q_heads, HD
    )
    queries = rotate(queries, my_position).astype(jnp.bfloat16).reshape(tok_rows, q_heads * HD)
    new_keys = jnp.dot(normed, w_key, preferred_element_type=jnp.float32).reshape(
        tok_rows, kv_heads, HD
    )
    new_keys = rotate(new_keys, my_position).astype(jnp.bfloat16)
    new_values = (
        jnp.dot(normed, w_value, preferred_element_type=jnp.float32)
        .astype(jnp.bfloat16)
        .reshape(tok_rows, kv_heads, HD)
    )
    extra = -(-tok_rows // 128) * 128 - tok_rows
    new_k = jnp.concatenate(
        [new_keys.reshape(tok_rows, HD), jnp.zeros((extra, HD), jnp.bfloat16)], axis=0
    )
    new_v = jnp.concatenate(
        [new_values.reshape(tok_rows, HD), jnp.zeros((extra, HD), jnp.bfloat16)], axis=0
    )
    new_req = jnp.concatenate([my_request, jnp.full((extra,), -1, jnp.int32)], axis=0)
    new_pos = jnp.concatenate([my_position, jnp.zeros((extra,), jnp.int32)], axis=0)
    slot_request, slot_position = slot_layout(block_of_shard[0], cache_keys.shape[0], cached_len)
    gathered = lax.all_gather(
        lax.all_gather(queries, SEQ[1], axis=0, tiled=True), SEQ[0], axis=0, tiled=True
    )
    average, log_weight = attend(
        gathered, request_all, position_all, cache_keys, cache_values, slot_request, slot_position,
        new_k, new_v, new_req, new_pos,
    )
    pairs = tok_rows * q_heads
    high = lax.reduce_precision(log_weight, exponent_bits=8, mantissa_bits=7)
    rest = log_weight - high
    middle = lax.reduce_precision(rest, exponent_bits=8, mantissa_bits=7)
    low = rest - middle
    packed = jnp.concatenate(
        [
            average.astype(jnp.bfloat16).reshape(seq_count, pairs * HD),
            high.astype(jnp.bfloat16).reshape(seq_count, pairs),
            middle.astype(jnp.bfloat16).reshape(seq_count, pairs),
            low.astype(jnp.bfloat16).reshape(seq_count, pairs),
        ],
        axis=1,
    )
    received = lax.all_to_all(packed, SEQ, 0, 0, tiled=True)
    part_avg = received[:, : pairs * HD].astype(jnp.float32)
    tail = received[:, pairs * HD :].astype(jnp.float32).reshape(seq_count, 3, pairs)
    part_log = tail[:, 0] + (tail[:, 1] + tail[:, 2])
    overall = jnp.max(part_log, axis=0, keepdims=True)
    factor = jnp.exp(part_log - overall)
    denominator = jnp.sum(factor, axis=0)
    spread = (
        jnp.arange(pairs, dtype=jnp.int32)[:, None]
        == (jnp.arange(pairs * HD, dtype=jnp.int32) // HD)[None, :]
    ).astype(jnp.float32)
    factor_wide = jnp.dot(factor, spread, precision=lax.Precision.HIGHEST)
    numerator = jnp.sum(part_avg * factor_wide, axis=0).reshape(pairs, HD)
    attended = (
        (numerator / denominator[:, None]).astype(jnp.bfloat16).reshape(tok_rows, q_heads * HD)
    )
    partial_out = jnp.dot(attended, w_out, preferred_element_type=jnp.float32)
    tp_count = lax.axis_size("tp")
    blocks = partial_out.astype(jnp.bfloat16).reshape(tok_rows, tp_count, -1).transpose(1, 0, 2)
    blocks = lax.all_to_all(blocks, "tp", 0, 0, tiled=True)
    return jnp.sum(blocks.astype(jnp.float32), axis=0).astype(jnp.bfloat16)


def split_mesh(mesh):
    seq_devices = mesh.devices[:, 0]
    try:
        hi = len({d.coords[1] for d in seq_devices})
    except AttributeError:
        hi = 4
    if seq_devices.shape[0] % hi:
        hi = 1
    lo = seq_devices.shape[0] // hi
    grid = mesh.devices.reshape(hi, lo, mesh.devices.shape[1])
    return Mesh(grid, (SEQ[0], SEQ[1], "tp"))


def solution(mesh):
    split = split_mesh(mesh)
    in_specs = (
        P(SEQ, None),
        P(),
        P(None, "tp"),
        P(None, "tp"),
        P(None, "tp"),
        P("tp", None),
        P(SEQ, "tp"),
        P(SEQ, "tp"),
        P(),
        P(SEQ),
    )
    out_specs = P(SEQ, "tp")
    return jax.shard_map(
        per_device, mesh=split, in_specs=in_specs, out_specs=out_specs, check_vma=False
    )
```

```python
import functools

import jax
import jax.numpy as jnp
from jax import lax
from jax.experimental import pallas as pl
from jax.sharding import Mesh, PartitionSpec as P

HD = 128
SPAN = 512
PREFILLS = 2


SEQ = ("seq_hi", "seq_lo")
NEGATIVE = -1e30
THETA = 1000000.0
EPSILON = 1e-06


def rotate(values, places):
    half_dim = values.shape[-1] // 2
    frequency = THETA ** (-jnp.arange(half_dim, dtype=jnp.float32) / half_dim)
    angles = places.astype(jnp.float32)[:, None] * frequency[None, :]
    cosine = jnp.cos(angles)[:, None, :]
    sine_part = jnp.sin(angles)[:, None, :]
    front_half = values[..., :half_dim]
    second = values[..., half_dim:]
    return jnp.concatenate(
        [front_half * cosine - second * sine_part, second * cosine + front_half * sine_part],
        axis=-1,
    )


def row_layout(row_count, cached_len):
    position_index = jnp.arange(row_count, dtype=jnp.int32)
    boundary = PREFILLS * SPAN
    request = jnp.where(
        position_index < boundary, position_index // SPAN, PREFILLS + position_index - boundary
    )
    offset = jnp.where(position_index < boundary, position_index % SPAN, 0)
    matches = request[:, None] == jnp.arange(cached_len.shape[0], dtype=jnp.int32)[None, :]
    begins = jnp.sum(jnp.where(matches, cached_len[None, :], 0), axis=1)
    return (request, begins + offset)


def slot_layout(block_number, slot_count, cached_len):
    packed = block_number * slot_count + jnp.arange(slot_count, dtype=jnp.int32)
    ending = jnp.cumsum(cached_len)
    before = packed[:, None] >= ending[None, :]
    request = jnp.sum(before.astype(jnp.int32), axis=1)
    places = packed - jnp.sum(jnp.where(before, cached_len[None, :], 0), axis=1)
    return (request, places)


def attend_kernel(
    q_ref, qr_ref, qp_ref, k_ref, v_ref, kr_ref, kp_ref, nk_ref, nv_ref, nr_ref, np_ref,
    avg_ref, lw_ref, *, heads
):
    seen_cache = qr_ref[...] == kr_ref[...]
    seen_new = (qr_ref[...] == nr_ref[...]) & (np_ref[...] <= qp_ref[...])
    tops = []
    for g in range(heads):
        qg = q_ref[:, g * HD:(g + 1) * HD]
        dims = (((1,), (1,)), ((), ()))
        cache_scores = lax.dot_general(
            qg, k_ref[...], dims, preferred_element_type=jnp.float32
        ) * HD ** (-0.5)
        new_scores = lax.dot_general(
            qg, nk_ref[...], dims, preferred_element_type=jnp.float32
        ) * HD ** (-0.5)
        cache_scores = jnp.where(seen_cache, cache_scores, NEGATIVE)
        new_scores = jnp.where(seen_new, new_scores, NEGATIVE)
        top = jnp.maximum(
            jnp.max(cache_scores, axis=1, keepdims=True), jnp.max(new_scores, axis=1, keepdims=True)
        )
        cache_weights = jnp.exp(cache_scores - top)
        new_weights = jnp.exp(new_scores - top)
        den = jnp.sum(cache_weights, axis=1, keepdims=True) + jnp.sum(
            new_weights, axis=1, keepdims=True
        )
        num = jnp.dot(
            cache_weights.astype(jnp.bfloat16), v_ref[...], preferred_element_type=jnp.float32
        ) + jnp.dot(new_weights.astype(jnp.bfloat16), nv_ref[...], preferred_element_type=jnp.float32)
        some = top > 0.5 * NEGATIVE
        avg_ref[:, g * HD:(g + 1) * HD] = jnp.where(some, num / den, 0.0).astype(avg_ref.dtype)
        tops.append(jnp.where(some, top + jnp.log(den), NEGATIVE))
    lw_ref[...] = jnp.concatenate(tops, axis=1)


def attend(q, q_req, q_pos, keys, values, k_req, k_pos, new_k, new_v, n_req, n_pos, block_rows=272):
    rows, width = q.shape
    heads = width // HD
    slots = keys.shape[0]
    fresh = new_k.shape[0]
    grid = (rows // block_rows,)
    row_block = lambda i: (i, 0)
    whole = lambda i: (0, 0)
    return pl.pallas_call(
        functools.partial(attend_kernel, heads=heads),
        grid=grid,
        in_specs=[
            pl.BlockSpec((block_rows, width), row_block),
            pl.BlockSpec((block_rows, 1), row_block),
            pl.BlockSpec((block_rows, 1), row_block),
            pl.BlockSpec((slots, HD), whole),
            pl.BlockSpec((slots, HD), whole),
            pl.BlockSpec((1, slots), whole),
            pl.BlockSpec((1, slots), whole),
            pl.BlockSpec((fresh, HD), whole),
            pl.BlockSpec((fresh, HD), whole),
            pl.BlockSpec((1, fresh), whole),
            pl.BlockSpec((1, fresh), whole),
        ],
        out_specs=[
            pl.BlockSpec((block_rows, width), row_block),
            pl.BlockSpec((block_rows, heads), row_block),
        ],
        out_shape=[
            jax.ShapeDtypeStruct((rows, width), jnp.bfloat16),
            jax.ShapeDtypeStruct((rows, heads), jnp.float32),
        ],
    )(
        q, q_req.reshape(rows, 1), q_pos.reshape(rows, 1), keys, values,
        k_req.reshape(1, slots), k_pos.reshape(1, slots),
        new_k, new_v, n_req.reshape(1, fresh), n_pos.reshape(1, fresh),
    )


def per_device(
    tokens,
    norm_gain,
    w_query,
    w_key,
    w_value,
    w_out,
    cache_keys,
    cache_values,
    cached_len,
    block_of_shard,
):
    seq_count = lax.axis_size(SEQ)
    seq_index = lax.axis_index(SEQ)
    tok_rows = tokens.shape[0]
    all_rows = tok_rows * seq_count
    q_heads = w_query.shape[1] // HD
    kv_heads = w_key.shape[1] // HD
    head_groups = q_heads // kv_heads
    boundary = PREFILLS * SPAN
    request_all, position_all = row_layout(all_rows, cached_len)
    my_request = lax.dynamic_slice_in_dim(request_all, seq_index * tok_rows, tok_rows)
    my_position = lax.dynamic_slice_in_dim(position_all, seq_index * tok_rows, tok_rows)
    hidden = tokens.astype(jnp.float32)
    scale_row = lax.rsqrt(jnp.mean(hidden * hidden, axis=1, keepdims=True) + EPSILON)
    normed = (hidden * scale_row * norm_gain.astype(jnp.float32)[None, :]).astype(jnp.bfloat16)
    queries = jnp.dot(normed, w_query, preferred_element_type=jnp.float32).reshape(
        tok_rows, q_heads, HD
    )
    queries = rotate(queries, my_position).astype(jnp.bfloat16).reshape(tok_rows, q_heads * HD)
    new_keys = jnp.dot(normed, w_key, preferred_element_type=jnp.float32).reshape(
        tok_rows, kv_heads, HD
    )
    new_keys = rotate(new_keys, my_position).astype(jnp.bfloat16)
    new_values = (
        jnp.dot(normed, w_value, preferred_element_type=jnp.float32)
        .astype(jnp.bfloat16)
        .reshape(tok_rows, kv_heads, HD)
    )
    extra = -(-tok_rows // 128) * 128 - tok_rows
    new_k = jnp.concatenate(
        [new_keys.reshape(tok_rows, HD), jnp.zeros((extra, HD), jnp.bfloat16)], axis=0
    )
    new_v = jnp.concatenate(
        [new_values.reshape(tok_rows, HD), jnp.zeros((extra, HD), jnp.bfloat16)], axis=0
    )
    new_req = jnp.concatenate([my_request, jnp.full((extra,), -1, jnp.int32)], axis=0)
    new_pos = jnp.concatenate([my_position, jnp.zeros((extra,), jnp.int32)], axis=0)
    slot_request, slot_position = slot_layout(block_of_shard[0], cache_keys.shape[0], cached_len)
    gathered = lax.all_gather(
        lax.all_gather(queries, SEQ[1], axis=0, tiled=True), SEQ[0], axis=0, tiled=True
    )
    average, log_weight = attend(
        gathered, request_all, position_all, cache_keys, cache_values, slot_request, slot_position,
        new_k, new_v, new_req, new_pos,
    )
    pairs = tok_rows * q_heads
    high = lax.reduce_precision(log_weight, exponent_bits=8, mantissa_bits=7)
    rest = log_weight - high
    middle = lax.reduce_precision(rest, exponent_bits=8, mantissa_bits=7)
    low = rest - middle
    packed = jnp.concatenate(
        [
            average.astype(jnp.bfloat16).reshape(seq_count, pairs * HD),
            high.astype(jnp.bfloat16).reshape(seq_count, pairs),
            middle.astype(jnp.bfloat16).reshape(seq_count, pairs),
            low.astype(jnp.bfloat16).reshape(seq_count, pairs),
            jnp.zeros((seq_count, -(-pairs * (HD + 3) // 256) * 256 - pairs * (HD + 3)), jnp.bfloat16),
        ],
        axis=1,
    )
    received = lax.all_to_all(packed, SEQ, 0, 0, tiled=True)
    part_avg = received[:, : pairs * HD].astype(jnp.float32)
    tail = received[:, pairs * HD : pairs * (HD + 3)].astype(jnp.float32).reshape(seq_count, 3, pairs)
    part_log = tail[:, 0] + (tail[:, 1] + tail[:, 2])
    overall = jnp.max(part_log, axis=0, keepdims=True)
    factor = jnp.exp(part_log - overall)
    denominator = jnp.sum(factor, axis=0)
    spread = (
        jnp.arange(pairs, dtype=jnp.int32)[:, None]
        == (jnp.arange(pairs * HD, dtype=jnp.int32) // HD)[None, :]
    ).astype(jnp.float32)
    factor_wide = jnp.dot(factor, spread, precision=lax.Precision.HIGHEST)
    numerator = jnp.sum(part_avg * factor_wide, axis=0).reshape(pairs, HD)
    attended = (
        (numerator / denominator[:, None]).astype(jnp.bfloat16).reshape(tok_rows, q_heads * HD)
    )
    partial_out = jnp.dot(attended, w_out, preferred_element_type=jnp.float32)
    tp_count = lax.axis_size("tp")
    blocks = partial_out.astype(jnp.bfloat16).reshape(tok_rows, tp_count, -1).transpose(1, 0, 2)
    blocks = lax.all_to_all(blocks, "tp", 0, 0, tiled=True)
    return jnp.sum(blocks.astype(jnp.float32), axis=0).astype(jnp.bfloat16)


def split_mesh(mesh):
    seq_devices = mesh.devices[:, 0]
    try:
        hi = len({d.coords[1] for d in seq_devices})
    except AttributeError:
        hi = 4
    if seq_devices.shape[0] % hi:
        hi = 1
    lo = seq_devices.shape[0] // hi
    grid = mesh.devices.reshape(hi, lo, mesh.devices.shape[1])
    return Mesh(grid, (SEQ[0], SEQ[1], "tp"))


def solution(mesh):
    split = split_mesh(mesh)
    in_specs = (
        P(SEQ, None),
        P(),
        P(None, "tp"),
        P(None, "tp"),
        P(None, "tp"),
        P("tp", None),
        P(SEQ, "tp"),
        P(SEQ, "tp"),
        P(),
        P(SEQ),
    )
    out_specs = P(SEQ, "tp")
    return jax.shard_map(
        per_device, mesh=split, in_specs=in_specs, out_specs=out_specs, check_vma=False
    )
```

```python
import functools

import jax
import jax.numpy as jnp
from jax import lax
from jax.experimental import pallas as pl
from jax.sharding import Mesh, PartitionSpec as P

HD = 128
SPAN = 512
PREFILLS = 2


SEQ = ("seq_hi", "seq_lo")
NEGATIVE = -1e30
THETA = 1000000.0
EPSILON = 1e-06


def rotate(values, places):
    half_dim = values.shape[-1] // 2
    frequency = THETA ** (-jnp.arange(half_dim, dtype=jnp.float32) / half_dim)
    angles = places.astype(jnp.float32)[:, None] * frequency[None, :]
    cosine = jnp.cos(angles)[:, None, :]
    sine_part = jnp.sin(angles)[:, None, :]
    front_half = values[..., :half_dim]
    second = values[..., half_dim:]
    return jnp.concatenate(
        [front_half * cosine - second * sine_part, second * cosine + front_half * sine_part],
        axis=-1,
    )


def row_layout(row_count, cached_len):
    position_index = jnp.arange(row_count, dtype=jnp.int32)
    boundary = PREFILLS * SPAN
    request = jnp.where(
        position_index < boundary, position_index // SPAN, PREFILLS + position_index - boundary
    )
    offset = jnp.where(position_index < boundary, position_index % SPAN, 0)
    matches = request[:, None] == jnp.arange(cached_len.shape[0], dtype=jnp.int32)[None, :]
    begins = jnp.sum(jnp.where(matches, cached_len[None, :], 0), axis=1)
    return (request, begins + offset)


def slot_layout(block_number, slot_count, cached_len):
    packed = block_number * slot_count + jnp.arange(slot_count, dtype=jnp.int32)
    ending = jnp.cumsum(cached_len)
    before = packed[:, None] >= ending[None, :]
    request = jnp.sum(before.astype(jnp.int32), axis=1)
    places = packed - jnp.sum(jnp.where(before, cached_len[None, :], 0), axis=1)
    return (request, places)


def attend_kernel(
    q_ref, qr_ref, qp_ref, k_ref, v_ref, kr_ref, kp_ref, nk_ref, nv_ref, nr_ref, np_ref,
    avg_ref, lw_ref, *, heads
):
    seen_cache = qr_ref[...] == kr_ref[...]
    seen_new = (qr_ref[...] == nr_ref[...]) & (np_ref[...] <= qp_ref[...])
    tops = []
    for g in range(heads):
        qg = q_ref[:, g * HD:(g + 1) * HD]
        dims = (((1,), (1,)), ((), ()))
        cache_scores = lax.dot_general(
            qg, k_ref[...], dims, preferred_element_type=jnp.float32
        ) * HD ** (-0.5)
        new_scores = lax.dot_general(
            qg, nk_ref[...], dims, preferred_element_type=jnp.float32
        ) * HD ** (-0.5)
        cache_scores = jnp.where(seen_cache, cache_scores, NEGATIVE)
        new_scores = jnp.where(seen_new, new_scores, NEGATIVE)
        top = jnp.maximum(
            jnp.max(cache_scores, axis=1, keepdims=True), jnp.max(new_scores, axis=1, keepdims=True)
        )
        cache_weights = jnp.exp(cache_scores - top)
        new_weights = jnp.exp(new_scores - top)
        den = jnp.sum(cache_weights, axis=1, keepdims=True) + jnp.sum(
            new_weights, axis=1, keepdims=True
        )
        num = jnp.dot(
            cache_weights.astype(jnp.bfloat16), v_ref[...], preferred_element_type=jnp.float32
        ) + jnp.dot(new_weights.astype(jnp.bfloat16), nv_ref[...], preferred_element_type=jnp.float32)
        some = top > 0.5 * NEGATIVE
        avg_ref[:, g * HD:(g + 1) * HD] = jnp.where(some, num / den, 0.0).astype(avg_ref.dtype)
        tops.append(jnp.where(some, top + jnp.log(den), NEGATIVE))
    lw_ref[...] = jnp.concatenate(tops, axis=1)


def attend(q, q_req, q_pos, keys, values, k_req, k_pos, new_k, new_v, n_req, n_pos, block_rows=544):
    rows, width = q.shape
    heads = width // HD
    slots = keys.shape[0]
    fresh = new_k.shape[0]
    grid = (rows // block_rows,)
    row_block = lambda i: (i, 0)
    whole = lambda i: (0, 0)
    return pl.pallas_call(
        functools.partial(attend_kernel, heads=heads),
        grid=grid,
        in_specs=[
            pl.BlockSpec((block_rows, width), row_block),
            pl.BlockSpec((block_rows, 1), row_block),
            pl.BlockSpec((block_rows, 1), row_block),
            pl.BlockSpec((slots, HD), whole),
            pl.BlockSpec((slots, HD), whole),
            pl.BlockSpec((1, slots), whole),
            pl.BlockSpec((1, slots), whole),
            pl.BlockSpec((fresh, HD), whole),
            pl.BlockSpec((fresh, HD), whole),
            pl.BlockSpec((1, fresh), whole),
            pl.BlockSpec((1, fresh), whole),
        ],
        out_specs=[
            pl.BlockSpec((block_rows, width), row_block),
            pl.BlockSpec((block_rows, heads), row_block),
        ],
        out_shape=[
            jax.ShapeDtypeStruct((rows, width), jnp.bfloat16),
            jax.ShapeDtypeStruct((rows, heads), jnp.float32),
        ],
    )(
        q, q_req.reshape(rows, 1), q_pos.reshape(rows, 1), keys, values,
        k_req.reshape(1, slots), k_pos.reshape(1, slots),
        new_k, new_v, n_req.reshape(1, fresh), n_pos.reshape(1, fresh),
    )


def per_device(
    tokens,
    norm_gain,
    w_query,
    w_key,
    w_value,
    w_out,
    cache_keys,
    cache_values,
    cached_len,
    block_of_shard,
):
    seq_count = lax.axis_size(SEQ)
    seq_index = lax.axis_index(SEQ)
    tok_rows = tokens.shape[0]
    all_rows = tok_rows * seq_count
    q_heads = w_query.shape[1] // HD
    kv_heads = w_key.shape[1] // HD
    head_groups = q_heads // kv_heads
    boundary = PREFILLS * SPAN
    request_all, position_all = row_layout(all_rows, cached_len)
    my_request = lax.dynamic_slice_in_dim(request_all, seq_index * tok_rows, tok_rows)
    my_position = lax.dynamic_slice_in_dim(position_all, seq_index * tok_rows, tok_rows)
    hidden = tokens.astype(jnp.float32)
    scale_row = lax.rsqrt(jnp.mean(hidden * hidden, axis=1, keepdims=True) + EPSILON)
    normed = (hidden * scale_row * norm_gain.astype(jnp.float32)[None, :]).astype(jnp.bfloat16)
    queries = jnp.dot(normed, w_query, preferred_element_type=jnp.float32).reshape(
        tok_rows, q_heads, HD
    )
    queries = rotate(queries, my_position).astype(jnp.bfloat16).reshape(tok_rows, q_heads * HD)
    new_keys = jnp.dot(normed, w_key, preferred_element_type=jnp.float32).reshape(
        tok_rows, kv_heads, HD
    )
    new_keys = rotate(new_keys, my_position).astype(jnp.bfloat16)
    new_values = (
        jnp.dot(normed, w_value, preferred_element_type=jnp.float32)
        .astype(jnp.bfloat16)
        .reshape(tok_rows, kv_heads, HD)
    )
    extra = -(-tok_rows // 128) * 128 - tok_rows
    new_k = jnp.concatenate(
        [new_keys.reshape(tok_rows, HD), jnp.zeros((extra, HD), jnp.bfloat16)], axis=0
    )
    new_v = jnp.concatenate(
        [new_values.reshape(tok_rows, HD), jnp.zeros((extra, HD), jnp.bfloat16)], axis=0
    )
    new_req = jnp.concatenate([my_request, jnp.full((extra,), -1, jnp.int32)], axis=0)
    new_pos = jnp.concatenate([my_position, jnp.zeros((extra,), jnp.int32)], axis=0)
    slot_request, slot_position = slot_layout(block_of_shard[0], cache_keys.shape[0], cached_len)
    gathered = lax.all_gather(
        lax.all_gather(queries, SEQ[1], axis=0, tiled=True), SEQ[0], axis=0, tiled=True
    )
    average, log_weight = attend(
        gathered, request_all, position_all, cache_keys, cache_values, slot_request, slot_position,
        new_k, new_v, new_req, new_pos,
    )
    pairs = tok_rows * q_heads
    high = lax.reduce_precision(log_weight, exponent_bits=8, mantissa_bits=7)
    rest = log_weight - high
    middle = lax.reduce_precision(rest, exponent_bits=8, mantissa_bits=7)
    low = rest - middle
    packed = jnp.concatenate(
        [
            average.astype(jnp.bfloat16).reshape(seq_count, pairs * HD),
            high.astype(jnp.bfloat16).reshape(seq_count, pairs),
            middle.astype(jnp.bfloat16).reshape(seq_count, pairs),
            low.astype(jnp.bfloat16).reshape(seq_count, pairs),
            jnp.zeros((seq_count, -(-pairs * (HD + 3) // 256) * 256 - pairs * (HD + 3)), jnp.bfloat16),
        ],
        axis=1,
    )
    received = lax.all_to_all(packed, SEQ, 0, 0, tiled=True)
    part_avg = received[:, : pairs * HD].astype(jnp.float32)
    tail = received[:, pairs * HD : pairs * (HD + 3)].astype(jnp.float32).reshape(seq_count, 3, pairs)
    part_log = tail[:, 0] + (tail[:, 1] + tail[:, 2])
    overall = jnp.max(part_log, axis=0, keepdims=True)
    factor = jnp.exp(part_log - overall)
    denominator = jnp.sum(factor, axis=0)
    spread = (
        jnp.arange(pairs, dtype=jnp.int32)[:, None]
        == (jnp.arange(pairs * HD, dtype=jnp.int32) // HD)[None, :]
    ).astype(jnp.float32)
    factor_wide = jnp.dot(factor, spread, precision=lax.Precision.HIGHEST)
    numerator = jnp.sum(part_avg * factor_wide, axis=0).reshape(pairs, HD)
    attended = (
        (numerator / denominator[:, None]).astype(jnp.bfloat16).reshape(tok_rows, q_heads * HD)
    )
    partial_out = jnp.dot(attended, w_out, preferred_element_type=jnp.float32)
    tp_count = lax.axis_size("tp")
    blocks = partial_out.astype(jnp.bfloat16).reshape(tok_rows, tp_count, -1).transpose(1, 0, 2)
    blocks = lax.all_to_all(blocks, "tp", 0, 0, tiled=True)
    return jnp.sum(blocks.astype(jnp.float32), axis=0).astype(jnp.bfloat16)


def split_mesh(mesh):
    seq_devices = mesh.devices[:, 0]
    try:
        hi = len({d.coords[1] for d in seq_devices})
    except AttributeError:
        hi = 4
    if seq_devices.shape[0] % hi:
        hi = 1
    lo = seq_devices.shape[0] // hi
    grid = mesh.devices.reshape(hi, lo, mesh.devices.shape[1])
    return Mesh(grid, (SEQ[0], SEQ[1], "tp"))


def solution(mesh):
    split = split_mesh(mesh)
    in_specs = (
        P(SEQ, None),
        P(),
        P(None, "tp"),
        P(None, "tp"),
        P(None, "tp"),
        P("tp", None),
        P(SEQ, "tp"),
        P(SEQ, "tp"),
        P(),
        P(SEQ),
    )
    out_specs = P(SEQ, "tp")
    return jax.shard_map(
        per_device, mesh=split, in_specs=in_specs, out_specs=out_specs, check_vma=False
    )
```

```python
import functools

import jax
import jax.numpy as jnp
from jax import lax
from jax.experimental import pallas as pl
from jax.sharding import Mesh, PartitionSpec as P

HD = 128
SPAN = 512
PREFILLS = 2


SEQ = ("seq_hi", "seq_lo")
NEGATIVE = -1e30
THETA = 1000000.0
EPSILON = 1e-06


def rotate(values, places):
    half_dim = values.shape[-1] // 2
    frequency = THETA ** (-jnp.arange(half_dim, dtype=jnp.float32) / half_dim)
    angles = places.astype(jnp.float32)[:, None] * frequency[None, :]
    cosine = jnp.cos(angles)[:, None, :]
    sine_part = jnp.sin(angles)[:, None, :]
    front_half = values[..., :half_dim]
    second = values[..., half_dim:]
    return jnp.concatenate(
        [front_half * cosine - second * sine_part, second * cosine + front_half * sine_part],
        axis=-1,
    )


def row_layout(row_count, cached_len):
    position_index = jnp.arange(row_count, dtype=jnp.int32)
    boundary = PREFILLS * SPAN
    request = jnp.where(
        position_index < boundary, position_index // SPAN, PREFILLS + position_index - boundary
    )
    offset = jnp.where(position_index < boundary, position_index % SPAN, 0)
    matches = request[:, None] == jnp.arange(cached_len.shape[0], dtype=jnp.int32)[None, :]
    begins = jnp.sum(jnp.where(matches, cached_len[None, :], 0), axis=1)
    return (request, begins + offset)


def slot_layout(block_number, slot_count, cached_len):
    packed = block_number * slot_count + jnp.arange(slot_count, dtype=jnp.int32)
    ending = jnp.cumsum(cached_len)
    before = packed[:, None] >= ending[None, :]
    request = jnp.sum(before.astype(jnp.int32), axis=1)
    places = packed - jnp.sum(jnp.where(before, cached_len[None, :], 0), axis=1)
    return (request, places)


def attend_kernel(
    q_ref, qr_ref, qp_ref, k_ref, v_ref, kr_ref, kp_ref, nk_ref, nv_ref, nr_ref, np_ref,
    avg_ref, lw_ref, *, heads
):
    seen_cache = qr_ref[...] == kr_ref[...]
    seen_new = (qr_ref[...] == nr_ref[...]) & (np_ref[...] <= qp_ref[...])
    tops = []
    for g in range(heads):
        qg = q_ref[:, g * HD:(g + 1) * HD]
        dims = (((1,), (1,)), ((), ()))
        cache_scores = lax.dot_general(
            qg, k_ref[...], dims, preferred_element_type=jnp.float32
        ) * HD ** (-0.5)
        new_scores = lax.dot_general(
            qg, nk_ref[...], dims, preferred_element_type=jnp.float32
        ) * HD ** (-0.5)
        cache_scores = jnp.where(seen_cache, cache_scores, NEGATIVE)
        new_scores = jnp.where(seen_new, new_scores, NEGATIVE)
        top = jnp.maximum(
            jnp.max(cache_scores, axis=1, keepdims=True), jnp.max(new_scores, axis=1, keepdims=True)
        )
        cache_weights = jnp.exp(cache_scores - top)
        new_weights = jnp.exp(new_scores - top)
        den = jnp.sum(cache_weights, axis=1, keepdims=True) + jnp.sum(
            new_weights, axis=1, keepdims=True
        )
        num = jnp.dot(
            cache_weights.astype(jnp.bfloat16), v_ref[...], preferred_element_type=jnp.float32
        ) + jnp.dot(new_weights.astype(jnp.bfloat16), nv_ref[...], preferred_element_type=jnp.float32)
        some = top > 0.5 * NEGATIVE
        avg_ref[:, g * HD:(g + 1) * HD] = jnp.where(some, num / den, 0.0).astype(avg_ref.dtype)
        tops.append(jnp.where(some, top + jnp.log(den), NEGATIVE))
    lw_ref[...] = jnp.concatenate(tops, axis=1)


def attend(q, q_req, q_pos, keys, values, k_req, k_pos, new_k, new_v, n_req, n_pos, block_rows=1088):
    rows, width = q.shape
    heads = width // HD
    slots = keys.shape[0]
    fresh = new_k.shape[0]
    grid = (rows // block_rows,)
    row_block = lambda i: (i, 0)
    whole = lambda i: (0, 0)
    return pl.pallas_call(
        functools.partial(attend_kernel, heads=heads),
        grid=grid,
        in_specs=[
            pl.BlockSpec((block_rows, width), row_block),
            pl.BlockSpec((block_rows, 1), row_block),
            pl.BlockSpec((block_rows, 1), row_block),
            pl.BlockSpec((slots, HD), whole),
            pl.BlockSpec((slots, HD), whole),
            pl.BlockSpec((1, slots), whole),
            pl.BlockSpec((1, slots), whole),
            pl.BlockSpec((fresh, HD), whole),
            pl.BlockSpec((fresh, HD), whole),
            pl.BlockSpec((1, fresh), whole),
            pl.BlockSpec((1, fresh), whole),
        ],
        out_specs=[
            pl.BlockSpec((block_rows, width), row_block),
            pl.BlockSpec((block_rows, heads), row_block),
        ],
        out_shape=[
            jax.ShapeDtypeStruct((rows, width), jnp.bfloat16),
            jax.ShapeDtypeStruct((rows, heads), jnp.float32),
        ],
    )(
        q, q_req.reshape(rows, 1), q_pos.reshape(rows, 1), keys, values,
        k_req.reshape(1, slots), k_pos.reshape(1, slots),
        new_k, new_v, n_req.reshape(1, fresh), n_pos.reshape(1, fresh),
    )


def per_device(
    tokens,
    norm_gain,
    w_query,
    w_key,
    w_value,
    w_out,
    cache_keys,
    cache_values,
    cached_len,
    block_of_shard,
):
    seq_count = lax.axis_size(SEQ)
    seq_index = lax.axis_index(SEQ)
    tok_rows = tokens.shape[0]
    all_rows = tok_rows * seq_count
    q_heads = w_query.shape[1] // HD
    kv_heads = w_key.shape[1] // HD
    head_groups = q_heads // kv_heads
    boundary = PREFILLS * SPAN
    request_all, position_all = row_layout(all_rows, cached_len)
    my_request = lax.dynamic_slice_in_dim(request_all, seq_index * tok_rows, tok_rows)
    my_position = lax.dynamic_slice_in_dim(position_all, seq_index * tok_rows, tok_rows)
    hidden = tokens.astype(jnp.float32)
    scale_row = lax.rsqrt(jnp.mean(hidden * hidden, axis=1, keepdims=True) + EPSILON)
    normed = (hidden * scale_row * norm_gain.astype(jnp.float32)[None, :]).astype(jnp.bfloat16)
    queries = jnp.dot(normed, w_query, preferred_element_type=jnp.float32).reshape(
        tok_rows, q_heads, HD
    )
    queries = rotate(queries, my_position).astype(jnp.bfloat16).reshape(tok_rows, q_heads * HD)
    new_keys = jnp.dot(normed, w_key, preferred_element_type=jnp.float32).reshape(
        tok_rows, kv_heads, HD
    )
    new_keys = rotate(new_keys, my_position).astype(jnp.bfloat16)
    new_values = (
        jnp.dot(normed, w_value, preferred_element_type=jnp.float32)
        .astype(jnp.bfloat16)
        .reshape(tok_rows, kv_heads, HD)
    )
    extra = -(-tok_rows // 128) * 128 - tok_rows
    new_k = jnp.concatenate(
        [new_keys.reshape(tok_rows, HD), jnp.zeros((extra, HD), jnp.bfloat16)], axis=0
    )
    new_v = jnp.concatenate(
        [new_values.reshape(tok_rows, HD), jnp.zeros((extra, HD), jnp.bfloat16)], axis=0
    )
    new_req = jnp.concatenate([my_request, jnp.full((extra,), -1, jnp.int32)], axis=0)
    new_pos = jnp.concatenate([my_position, jnp.zeros((extra,), jnp.int32)], axis=0)
    slot_request, slot_position = slot_layout(block_of_shard[0], cache_keys.shape[0], cached_len)
    gathered = lax.all_gather(
        lax.all_gather(queries, SEQ[1], axis=0, tiled=True), SEQ[0], axis=0, tiled=True
    )
    average, log_weight = attend(
        gathered, request_all, position_all, cache_keys, cache_values, slot_request, slot_position,
        new_k, new_v, new_req, new_pos,
    )
    pairs = tok_rows * q_heads
    high = lax.reduce_precision(log_weight, exponent_bits=8, mantissa_bits=7)
    rest = log_weight - high
    middle = lax.reduce_precision(rest, exponent_bits=8, mantissa_bits=7)
    low = rest - middle
    packed = jnp.concatenate(
        [
            average.astype(jnp.bfloat16).reshape(seq_count, pairs * HD),
            high.astype(jnp.bfloat16).reshape(seq_count, pairs),
            middle.astype(jnp.bfloat16).reshape(seq_count, pairs),
            low.astype(jnp.bfloat16).reshape(seq_count, pairs),
            jnp.zeros((seq_count, -(-pairs * (HD + 3) // 256) * 256 - pairs * (HD + 3)), jnp.bfloat16),
        ],
        axis=1,
    )
    received = lax.all_to_all(packed, SEQ, 0, 0, tiled=True)
    part_avg = received[:, : pairs * HD].astype(jnp.float32)
    tail = received[:, pairs * HD : pairs * (HD + 3)].astype(jnp.float32).reshape(seq_count, 3, pairs)
    part_log = tail[:, 0] + (tail[:, 1] + tail[:, 2])
    overall = jnp.max(part_log, axis=0, keepdims=True)
    factor = jnp.exp(part_log - overall)
    denominator = jnp.sum(factor, axis=0)
    spread = (
        jnp.arange(pairs, dtype=jnp.int32)[:, None]
        == (jnp.arange(pairs * HD, dtype=jnp.int32) // HD)[None, :]
    ).astype(jnp.float32)
    factor_wide = jnp.dot(factor, spread, precision=lax.Precision.HIGHEST)
    numerator = jnp.sum(part_avg * factor_wide, axis=0).reshape(pairs, HD)
    attended = (
        (numerator / denominator[:, None]).astype(jnp.bfloat16).reshape(tok_rows, q_heads * HD)
    )
    partial_out = jnp.dot(attended, w_out, preferred_element_type=jnp.float32)
    tp_count = lax.axis_size("tp")
    blocks = partial_out.astype(jnp.bfloat16).reshape(tok_rows, tp_count, -1).transpose(1, 0, 2)
    blocks = lax.all_to_all(blocks, "tp", 0, 0, tiled=True)
    return jnp.sum(blocks.astype(jnp.float32), axis=0).astype(jnp.bfloat16)


def split_mesh(mesh):
    seq_devices = mesh.devices[:, 0]
    try:
        hi = len({d.coords[1] for d in seq_devices})
    except AttributeError:
        hi = 4
    if seq_devices.shape[0] % hi:
        hi = 1
    lo = seq_devices.shape[0] // hi
    grid = mesh.devices.reshape(hi, lo, mesh.devices.shape[1])
    return Mesh(grid, (SEQ[0], SEQ[1], "tp"))


def solution(mesh):
    split = split_mesh(mesh)
    in_specs = (
        P(SEQ, None),
        P(),
        P(None, "tp"),
        P(None, "tp"),
        P(None, "tp"),
        P("tp", None),
        P(SEQ, "tp"),
        P(SEQ, "tp"),
        P(),
        P(SEQ),
    )
    out_specs = P(SEQ, "tp")
    return jax.shard_map(
        per_device, mesh=split, in_specs=in_specs, out_specs=out_specs, check_vma=False
    )
```

```python
import functools

import jax
import jax.numpy as jnp
from jax import lax
from jax.experimental import pallas as pl
from jax.sharding import Mesh, PartitionSpec as P

HD = 128
SPAN = 512
PREFILLS = 2


SEQ = ("seq_hi", "seq_lo")
NEGATIVE = -1e30
THETA = 1000000.0
EPSILON = 1e-06


def rotate(values, places):
    half_dim = values.shape[-1] // 2
    frequency = THETA ** (-jnp.arange(half_dim, dtype=jnp.float32) / half_dim)
    angles = places.astype(jnp.float32)[:, None] * frequency[None, :]
    cosine = jnp.cos(angles)[:, None, :]
    sine_part = jnp.sin(angles)[:, None, :]
    front_half = values[..., :half_dim]
    second = values[..., half_dim:]
    return jnp.concatenate(
        [front_half * cosine - second * sine_part, second * cosine + front_half * sine_part],
        axis=-1,
    )


def row_layout(row_count, cached_len):
    position_index = jnp.arange(row_count, dtype=jnp.int32)
    boundary = PREFILLS * SPAN
    request = jnp.where(
        position_index < boundary, position_index // SPAN, PREFILLS + position_index - boundary
    )
    offset = jnp.where(position_index < boundary, position_index % SPAN, 0)
    matches = request[:, None] == jnp.arange(cached_len.shape[0], dtype=jnp.int32)[None, :]
    begins = jnp.sum(jnp.where(matches, cached_len[None, :], 0), axis=1)
    return (request, begins + offset)


def slot_layout(block_number, slot_count, cached_len):
    packed = block_number * slot_count + jnp.arange(slot_count, dtype=jnp.int32)
    ending = jnp.cumsum(cached_len)
    before = packed[:, None] >= ending[None, :]
    request = jnp.sum(before.astype(jnp.int32), axis=1)
    places = packed - jnp.sum(jnp.where(before, cached_len[None, :], 0), axis=1)
    return (request, places)


def attend_kernel(
    q_ref, qr_ref, qp_ref, k_ref, v_ref, kr_ref, nk_ref, nv_ref, nr_ref, np_ref,
    avg_ref, lw_ref, *, heads
):
    seen_cache = qr_ref[...] == kr_ref[...]
    seen_new = (qr_ref[...] == nr_ref[...]) & (np_ref[...] <= qp_ref[...])
    tops = []
    for g in range(heads):
        qg = q_ref[:, g * HD:(g + 1) * HD]
        dims = (((1,), (1,)), ((), ()))
        cache_scores = lax.dot_general(
            qg, k_ref[...], dims, preferred_element_type=jnp.float32
        ) * HD ** (-0.5)
        new_scores = lax.dot_general(
            qg, nk_ref[...], dims, preferred_element_type=jnp.float32
        ) * HD ** (-0.5)
        cache_scores = jnp.where(seen_cache, cache_scores, NEGATIVE)
        new_scores = jnp.where(seen_new, new_scores, NEGATIVE)
        top = jnp.maximum(
            jnp.max(cache_scores, axis=1, keepdims=True), jnp.max(new_scores, axis=1, keepdims=True)
        )
        cache_weights = jnp.exp(cache_scores - top)
        new_weights = jnp.exp(new_scores - top)
        den = jnp.sum(cache_weights, axis=1, keepdims=True) + jnp.sum(
            new_weights, axis=1, keepdims=True
        )
        num = jnp.dot(
            cache_weights.astype(jnp.bfloat16), v_ref[...], preferred_element_type=jnp.float32
        ) + jnp.dot(new_weights.astype(jnp.bfloat16), nv_ref[...], preferred_element_type=jnp.float32)
        some = top > 0.5 * NEGATIVE
        avg_ref[:, g * HD:(g + 1) * HD] = jnp.where(some, num / den, 0.0).astype(avg_ref.dtype)
        tops.append(jnp.where(some, top + jnp.log(den), NEGATIVE))
    lw_ref[...] = jnp.concatenate(tops, axis=1)


def attend(q, q_req, q_pos, keys, values, k_req, new_k, new_v, n_req, n_pos, block_rows=544):
    rows, width = q.shape
    heads = width // HD
    slots = keys.shape[0]
    fresh = new_k.shape[0]
    grid = (rows // block_rows,)
    row_block = lambda i: (i, 0)
    whole = lambda i: (0, 0)
    return pl.pallas_call(
        functools.partial(attend_kernel, heads=heads),
        grid=grid,
        in_specs=[
            pl.BlockSpec((block_rows, width), row_block),
            pl.BlockSpec((block_rows, 1), row_block),
            pl.BlockSpec((block_rows, 1), row_block),
            pl.BlockSpec((slots, HD), whole),
            pl.BlockSpec((slots, HD), whole),
            pl.BlockSpec((1, slots), whole),
            pl.BlockSpec((fresh, HD), whole),
            pl.BlockSpec((fresh, HD), whole),
            pl.BlockSpec((1, fresh), whole),
            pl.BlockSpec((1, fresh), whole),
        ],
        out_specs=[
            pl.BlockSpec((block_rows, width), row_block),
            pl.BlockSpec((block_rows, heads), row_block),
        ],
        out_shape=[
            jax.ShapeDtypeStruct((rows, width), jnp.bfloat16),
            jax.ShapeDtypeStruct((rows, heads), jnp.float32),
        ],
    )(
        q, q_req.reshape(rows, 1), q_pos.reshape(rows, 1), keys, values,
        k_req.reshape(1, slots),
        new_k, new_v, n_req.reshape(1, fresh), n_pos.reshape(1, fresh),
    )


def per_device(
    tokens,
    norm_gain,
    w_query,
    w_key,
    w_value,
    w_out,
    cache_keys,
    cache_values,
    cached_len,
    block_of_shard,
):
    seq_count = lax.axis_size(SEQ)
    seq_index = lax.axis_index(SEQ)
    tok_rows = tokens.shape[0]
    all_rows = tok_rows * seq_count
    q_heads = w_query.shape[1] // HD
    kv_heads = w_key.shape[1] // HD
    head_groups = q_heads // kv_heads
    boundary = PREFILLS * SPAN
    request_all, position_all = row_layout(all_rows, cached_len)
    my_request = lax.dynamic_slice_in_dim(request_all, seq_index * tok_rows, tok_rows)
    my_position = lax.dynamic_slice_in_dim(position_all, seq_index * tok_rows, tok_rows)
    hidden = tokens.astype(jnp.float32)
    scale_row = lax.rsqrt(jnp.mean(hidden * hidden, axis=1, keepdims=True) + EPSILON)
    normed = (hidden * scale_row * norm_gain.astype(jnp.float32)[None, :]).astype(jnp.bfloat16)
    queries = jnp.dot(normed, w_query, preferred_element_type=jnp.float32).reshape(
        tok_rows, q_heads, HD
    )
    queries = rotate(queries, my_position).astype(jnp.bfloat16).reshape(tok_rows, q_heads * HD)
    new_keys = jnp.dot(normed, w_key, preferred_element_type=jnp.float32).reshape(
        tok_rows, kv_heads, HD
    )
    new_keys = rotate(new_keys, my_position).astype(jnp.bfloat16)
    new_values = (
        jnp.dot(normed, w_value, preferred_element_type=jnp.float32)
        .astype(jnp.bfloat16)
        .reshape(tok_rows, kv_heads, HD)
    )
    extra = -(-tok_rows // 128) * 128 - tok_rows
    new_k = jnp.concatenate(
        [new_keys.reshape(tok_rows, HD), jnp.zeros((extra, HD), jnp.bfloat16)], axis=0
    )
    new_v = jnp.concatenate(
        [new_values.reshape(tok_rows, HD), jnp.zeros((extra, HD), jnp.bfloat16)], axis=0
    )
    new_req = jnp.concatenate([my_request, jnp.full((extra,), -1, jnp.int32)], axis=0)
    new_pos = jnp.concatenate([my_position, jnp.zeros((extra,), jnp.int32)], axis=0)
    slot_request, _ = slot_layout(block_of_shard[0], cache_keys.shape[0], cached_len)
    gathered = lax.all_gather(
        lax.all_gather(queries, SEQ[1], axis=0, tiled=True), SEQ[0], axis=0, tiled=True
    )
    average, log_weight = attend(
        gathered, request_all, position_all, cache_keys, cache_values, slot_request,
        new_k, new_v, new_req, new_pos,
    )
    pairs = tok_rows * q_heads
    high = lax.reduce_precision(log_weight, exponent_bits=8, mantissa_bits=7)
    rest = log_weight - high
    middle = lax.reduce_precision(rest, exponent_bits=8, mantissa_bits=7)
    low = rest - middle
    packed = jnp.concatenate(
        [
            average.astype(jnp.bfloat16).reshape(seq_count, pairs * HD),
            high.astype(jnp.bfloat16).reshape(seq_count, pairs),
            middle.astype(jnp.bfloat16).reshape(seq_count, pairs),
            low.astype(jnp.bfloat16).reshape(seq_count, pairs),
            jnp.zeros((seq_count, -(-pairs * (HD + 3) // 256) * 256 - pairs * (HD + 3)), jnp.bfloat16),
        ],
        axis=1,
    )
    received = lax.all_to_all(packed, SEQ, 0, 0, tiled=True)
    part_avg = received[:, : pairs * HD].astype(jnp.float32)
    tail = received[:, pairs * HD : pairs * (HD + 3)].astype(jnp.float32).reshape(seq_count, 3, pairs)
    part_log = tail[:, 0] + (tail[:, 1] + tail[:, 2])
    overall = jnp.max(part_log, axis=0, keepdims=True)
    factor = jnp.exp(part_log - overall)
    denominator = jnp.sum(factor, axis=0)
    spread = (
        jnp.arange(pairs, dtype=jnp.int32)[:, None]
        == (jnp.arange(pairs * HD, dtype=jnp.int32) // HD)[None, :]
    ).astype(jnp.float32)
    factor_wide = jnp.dot(factor, spread, precision=lax.Precision.HIGHEST)
    numerator = jnp.sum(part_avg * factor_wide, axis=0).reshape(pairs, HD)
    attended = (
        (numerator / denominator[:, None]).astype(jnp.bfloat16).reshape(tok_rows, q_heads * HD)
    )
    partial_out = jnp.dot(attended, w_out, preferred_element_type=jnp.float32)
    tp_count = lax.axis_size("tp")
    blocks = partial_out.astype(jnp.bfloat16).reshape(tok_rows, tp_count, -1).transpose(1, 0, 2)
    blocks = lax.all_to_all(blocks, "tp", 0, 0, tiled=True)
    return jnp.sum(blocks.astype(jnp.float32), axis=0).astype(jnp.bfloat16)


def split_mesh(mesh):
    seq_devices = mesh.devices[:, 0]
    try:
        hi = len({d.coords[1] for d in seq_devices})
    except AttributeError:
        hi = 4
    if seq_devices.shape[0] % hi:
        hi = 1
    lo = seq_devices.shape[0] // hi
    grid = mesh.devices.reshape(hi, lo, mesh.devices.shape[1])
    return Mesh(grid, (SEQ[0], SEQ[1], "tp"))


def solution(mesh):
    split = split_mesh(mesh)
    in_specs = (
        P(SEQ, None),
        P(),
        P(None, "tp"),
        P(None, "tp"),
        P(None, "tp"),
        P("tp", None),
        P(SEQ, "tp"),
        P(SEQ, "tp"),
        P(),
        P(SEQ),
    )
    out_specs = P(SEQ, "tp")
    return jax.shard_map(
        per_device, mesh=split, in_specs=in_specs, out_specs=out_specs, check_vma=False
    )
```
